32 devices in a mesh: tm: 16 (over z, y, x), sec: 2 (over core).
Axes of the slice: x: 2, y: 2, z: 4, core: 2. Of those that a mesh axis runs over, the one named last changes fastest.
Arguments:
- signal: bfloat16 [2048, 16384], P('sec', 'tm')
- round_shard: int32 [2], replicated, may hold values from 0 to 15
- offsets: int32 [2, 16], replicated, may hold values from 0 to 896
- chan_range: int32 [2, 16, 2], replicated, may hold values from 0 to 2048, as said below
Outputs:
- detection: float32 [2, 16, 16384], P(None, None, 'tm')
The draws below stay inside these ranges and needn't reach their ends.
Inputs may be any that keep to these rules, and one draw needn't show every extreme that they name: chan_range[r, k] = (lo, hi) with lo < hi and hi - lo >= 512.
All inputs are finite; a program needn't handle non-finite values.
Results may differ from the reference program's by a relative error of at most 0.0003.
Values may be sent and summed in bfloat16 or wider, within the bound.
No kernel may reach another device: no remote copies, remote signals or barrier semaphores. Data moves between devices by JAX's collectives and lax.ppermute only.
A program may use at most 64 MiB of HBM per device.

```python
import math
import jax
import jax.numpy as jnp
from jax import lax

CH = 2048
L = 128
K = 16
TPL_BLOCK = 4
ROUNDS = 2
T_DEV = 1024
S = 16384
N_TM = 16


def draw_signal(key, part):
    key_chan, key_time, key_noise = jax.random.split(key, 3)
    chan_scale = jnp.exp(jax.random.uniform(key_chan, (CH, 1), jnp.float32, 0.0, math.log(10.0)))
    time_scale = jnp.exp(jax.random.uniform(key_time, (1, S), jnp.float32, 0.0, math.log(10.0)))
    base = jax.random.normal(key_noise, (CH, S), jnp.float32)
    return (base * chan_scale * time_scale).astype(jnp.bfloat16)


def draw_chan_range(key, part):
    key_low, key_width = jax.random.split(jax.random.fold_in(key, 7), 2)
    lower = jnp.maximum(jax.random.randint(key_low, (ROUNDS, K), -(CH // 4), CH // 2 + 1), 0)
    width = jax.random.randint(key_width, (ROUNDS, K), CH // 4, CH + 1)
    upper = jnp.minimum(lower + width, CH)
    return jnp.stack([lower, upper], axis=-1).astype(jnp.int32)


def with_ends(result, own_key, low, top_value):
    longest = result.shape.index(max(result.shape))
    spots = []
    for shift in (0, 1):
        where = [jax.random.randint(jax.random.fold_in(own_key, axis), (), 0, length) for axis, length in enumerate(result.shape)]
        where[longest] = (where[longest] + shift) % result.shape[longest]
        spots.append(tuple(where))
    return result.at[spots[0]].set(low).at[spots[1]].set(top_value)


def setup_inputs(seed: int = 0) -> dict:
    seeds = jax.random.split(jax.random.key(seed), 5)
    signal = draw_signal(jax.random.fold_in(seeds[4], 71), 0)
    round_shard = jax.random.randint(seeds[1], (ROUNDS,), 0, N_TM).astype(jnp.int32)
    offsets = with_ends(jax.random.randint(seeds[2], (ROUNDS, K), 0, T_DEV - L + 1), jax.random.fold_in(seeds[2], 1), 0, T_DEV - L).astype(jnp.int32)
    chan_range = draw_chan_range(jax.random.fold_in(seeds[4], 71), 0)
    return {"signal": signal, "round_shard": round_shard, "offsets": offsets, "chan_range": chan_range}


EPS = 1e-06

def skew_sum(product, lag_count):
    group_count, tap_count, span_width = product.shape
    flipped = product[:, :, ::-1]
    widened = jnp.pad(flipped, ((0, 0), (0, 0), (0, 1)))
    sheared = widened.reshape(group_count, tap_count * (span_width + 1))[:, :tap_count * span_width]
    sheared = sheared.reshape(group_count, tap_count, span_width)
    summed = lax.optimization_barrier(jnp.sum(sheared, axis=1))
    return summed[:, span_width - lag_count:][:, ::-1]

def correlate(templates, extended, lag_count):
    template_count = templates.shape[0]
    grouped = templates.reshape(template_count // TPL_BLOCK, TPL_BLOCK, templates.shape[1], templates.shape[2])

    def one_block(block):
        product = jnp.einsum('kcl,cw->klw', block.astype(jnp.float32), extended.astype(jnp.float32), preferred_element_type=jnp.float32)
        return skew_sum(product, lag_count)
    return lax.map(one_block, grouped).reshape(template_count, lag_count)

def sliding_energy(masks, extended, lag_count, tap_count):
    squares = jnp.square(extended.astype(jnp.float32))
    summed = jnp.dot(masks, squares, precision=lax.Precision.HIGHEST, preferred_element_type=jnp.float32)
    running = jnp.pad(jnp.cumsum(summed, axis=1), ((0, 0), (1, 0)))
    return running[:, tap_count:tap_count + lag_count] - running[:, :lag_count]

def reference(signal, round_shard, offsets, chan_range):
    padded = jnp.concatenate([signal, jnp.zeros((CH, L), signal.dtype)], axis=1)
    channel = jnp.arange(CH, dtype=jnp.int32)
    results = []
    for level in range(ROUNDS):
        root = round_shard[level].astype(jnp.int32)
        starts = (root * T_DEV + offsets[level]).astype(jnp.int32)
        windows = jax.vmap(lambda first: lax.dynamic_slice_in_dim(signal, first, L, axis=1))(starts)
        lower = chan_range[level, :, 0]
        upper = chan_range[level, :, 1]
        inside = (channel[None, :] >= lower[:, None]) & (channel[None, :] < upper[:, None])
        masks = inside.astype(jnp.float32)
        templates = jnp.where(inside[:, :, None], windows, jnp.zeros_like(windows))
        tpower = lax.optimization_barrier(jnp.sum(jnp.square(templates.astype(jnp.float32)), axis=(1, 2)))

        def one_time(block_index):
            extended = lax.dynamic_slice_in_dim(padded, (block_index * T_DEV).astype(jnp.int32), T_DEV + L, axis=1)
            return (correlate(templates, extended, T_DEV), sliding_energy(masks, extended, T_DEV, L))
        corr_blocks, energy_blocks = lax.map(one_time, jnp.arange(N_TM, dtype=jnp.int32))
        corr = jnp.transpose(corr_blocks, (1, 0, 2)).reshape(K, S)
        energy = jnp.transpose(energy_blocks, (1, 0, 2)).reshape(K, S)
        normed = corr / jnp.sqrt(energy * tpower[:, None] + EPS)
        meansq = lax.optimization_barrier(jnp.sum(normed * normed, axis=1)) / S
        results.append(normed / jnp.sqrt(meansq[:, None] + EPS))
    return jnp.stack(results, axis=0)
```

```python
import jax
import jax.numpy as jnp
from jax import lax
from jax.experimental import pallas as pl
from jax.experimental.pallas import tpu as pltpu
from jax.sharding import PartitionSpec as P

L = 128
GROUP = 4

EPS = 1e-06


def from_behind(value, axis, by):
    length = lax.axis_size(axis)
    pairs = [(i, i + by) for i in range(length) if 0 <= i + by < length]
    return lax.ppermute(value, axis, pairs)


def butterfly_sum(value, axis):
    size = lax.axis_size(axis)
    if size & (size - 1):
        return lax.psum(value, axis)
    step = 1
    while step < size:
        value = value + lax.ppermute(value, axis, [(i, i ^ step) for i in range(size)])
        step *= 2
    return value


def correlate_kernel(tmpl_ref, ext_ref, out_ref):
    width = ext_ref.shape[1]
    lags = out_ref.shape[2]
    group, taps, chans = tmpl_ref.shape
    product = jnp.dot(
        tmpl_ref[...].reshape(group * taps, chans), ext_ref[...], preferred_element_type=jnp.float32
    )
    for g in range(group):
        rows = product[g * taps : (g + 1) * taps]
        sheared = pltpu.roll(rows, width - (taps - 1), 1, stride=1, stride_axis=0)
        out_ref[0, g : g + 1, :] = jnp.sum(sheared, axis=0, keepdims=True)[:, :lags]


def correlate(templates, extended, lag_count):
    count, taps, chans = templates.shape
    width = extended.shape[1]
    steps = count // GROUP
    cost = pl.CostEstimate(
        flops=2 * count * taps * chans * width,
        transcendentals=0,
        bytes_accessed=templates.size * 2 + extended.size * 2 + count * lag_count * 4,
    )
    out = pl.pallas_call(
        correlate_kernel,
        grid=(steps,),
        in_specs=[
            pl.BlockSpec((GROUP, taps, chans), lambda i: (i, 0, 0)),
            pl.BlockSpec((chans, width), lambda i: (0, 0)),
        ],
        out_specs=pl.BlockSpec((1, GROUP, lag_count), lambda i: (i, 0, 0)),
        out_shape=jax.ShapeDtypeStruct((steps, GROUP, lag_count), jnp.float32),
        cost_estimate=cost,
    )(templates, extended)
    return out.reshape(count, lag_count)


def window_sum(values, taps, lag_count):
    span = 1
    while span < taps:
        values = values[:, :-span] + values[:, span:]
        span *= 2
    return values[:, :lag_count]


def shards(signal, round_shard, offsets, chan_range):
    chan_local, lag_count = signal.shape
    rounds, count = offsets.shape
    section = lax.axis_index("sec")
    place = lax.axis_index("tm")
    total_lags = lag_count * lax.axis_size("tm")

    right_rim = from_behind(signal[:, :L], "tm", -1)
    extended = jnp.concatenate([signal, right_rim], axis=1)
    channel = section * chan_local + jnp.arange(chan_local, dtype=jnp.int32)
    lower = chan_range[:, :, 0]
    upper = chan_range[:, :, 1]
    inside = (channel >= lower[:, :, None]) & (channel < upper[:, :, None])

    flipped = jnp.transpose(signal)[::-1]
    own = place == round_shard
    blocks = jnp.where(own[:, None, None], flipped[None], jnp.zeros_like(flipped)[None])
    blocks = lax.psum(blocks, "tm")
    starts = (lag_count - L) - offsets
    rows = [
        lax.dynamic_slice_in_dim(blocks[r], starts[r, k], L, axis=0)
        for r in range(rounds)
        for k in range(count)
    ]
    templates = jnp.stack(rows).reshape(rounds, count, L, chan_local)
    templates = jnp.where(inside[:, :, None, :], templates, jnp.zeros_like(templates))
    templates = templates.reshape(rounds * count, L, chan_local)
    local_power = jnp.sum(jnp.square(templates.astype(jnp.float32)), axis=(1, 2))
    tmpl_power = butterfly_sum(local_power, "sec")

    squares = jnp.square(extended.astype(jnp.float32))
    high = lax.reduce_precision(squares, exponent_bits=8, mantissa_bits=7)
    low = (squares - high).astype(jnp.bfloat16)
    masks = inside.reshape(rounds * count, chan_local).astype(jnp.bfloat16)
    summed = jnp.dot(masks, high.astype(jnp.bfloat16), preferred_element_type=jnp.float32)
    summed = summed + jnp.dot(masks, low, preferred_element_type=jnp.float32)
    energy_local = window_sum(summed, L, lag_count)

    corr_local = correlate(templates, extended, lag_count)
    both = butterfly_sum(jnp.stack([corr_local, energy_local]), "sec")
    corr, energy = both[0], both[1]
    normed = corr / jnp.sqrt(energy * tmpl_power[:, None] + EPS)
    power_sum = butterfly_sum(jnp.sum(normed * normed, axis=1), "tm")
    meansq = power_sum / total_lags
    scored = normed / jnp.sqrt(meansq[:, None] + EPS)
    return scored.reshape(rounds, count, lag_count)


def solution(mesh):
    placed = (P("sec", "tm"), P(), P(), P())
    return jax.shard_map(
        shards, mesh=mesh, in_specs=placed, out_specs=P(None, None, "tm"), check_vma=False
    )
```

```python
import jax
import jax.numpy as jnp
from jax import lax
from jax.experimental import pallas as pl
from jax.experimental.pallas import tpu as pltpu
from jax.sharding import PartitionSpec as P

L = 128
GROUP = 4
REACH = L + 16

EPS = 1e-06


def from_behind(value, axis, by):
    length = lax.axis_size(axis)
    pairs = [(i, i + by) for i in range(length) if 0 <= i + by < length]
    return lax.ppermute(value, axis, pairs)


def group_sum(value, axis):
    size = lax.axis_size(axis)
    place = lax.axis_index(axis)
    stride = 1
    while stride < size:
        fan = 4 if size % (stride * 4) == 0 else 2 if size % (stride * 2) == 0 else 0
        if fan == 0:
            return lax.psum(value, axis)
        member = (place // stride) % fan
        got = {0: value}
        for d in range(1, fan):
            pairs = [(i, i ^ (d * stride)) for i in range(size)]
            got[d] = lax.ppermute(value, axis, pairs)
        total = None
        for m in range(fan):
            part = got[0]
            for d in range(1, fan):
                part = jnp.where((member ^ d) == m, got[d], part)
            total = part if total is None else total + part
        value = total
        stride *= fan
    return value


def correlate_kernel(meta_ref, blk_ref, ext_ref, corr_ref, power_ref):
    step = pl.program_id(0)
    chans = blk_ref.shape[2]
    width = ext_ref.shape[1]
    group = corr_ref.shape[1]
    lags = corr_ref.shape[2]
    tap = lax.broadcasted_iota(jnp.int32, (L, REACH), 0)
    col = lax.broadcasted_iota(jnp.int32, (L, REACH), 1)
    lane = lax.broadcasted_iota(jnp.int32, (L, chans), 1)
    pieces = []
    for g in range(group):
        idx = step * group + g
        first = meta_ref[4 * idx]
        shift = meta_ref[4 * idx + 1]
        lower = meta_ref[4 * idx + 2]
        upper = meta_ref[4 * idx + 3]
        rows = blk_ref[0, pl.ds(pl.multiple_of(first, 16), REACH), :]
        pick = (col == shift + (L - 1) - tap).astype(jnp.bfloat16)
        chosen = jnp.dot(pick, rows, preferred_element_type=jnp.float32)
        chosen = jnp.where((lane >= lower) & (lane < upper), chosen, 0.0)
        power_ref[0, g : g + 1, :] = jnp.full((1, 128), jnp.sum(chosen * chosen), jnp.float32)
        pieces.append(chosen.astype(jnp.bfloat16))
    product = jnp.dot(
        jnp.concatenate(pieces, axis=0), ext_ref[...], preferred_element_type=jnp.float32
    )
    for g in range(group):
        rows = product[g * L : (g + 1) * L]
        sheared = pltpu.roll(rows, width - (L - 1), 1, stride=1, stride_axis=0)
        corr_ref[0, g : g + 1, :] = jnp.sum(sheared, axis=0, keepdims=True)[:, :lags]


def correlate(meta, blocks, extended, count):
    rounds, span, chans = blocks.shape
    width = extended.shape[1]
    lag_count = span
    steps = rounds * count // GROUP
    per_round = count // GROUP
    cost = pl.CostEstimate(
        flops=2 * rounds * count * L * (chans * width + REACH * chans),
        transcendentals=0,
        bytes_accessed=blocks.size * 2 + extended.size * 2 + rounds * count * lag_count * 4,
    )
    grid_spec = pltpu.PrefetchScalarGridSpec(
        num_scalar_prefetch=1,
        grid=(steps,),
        in_specs=[
            pl.BlockSpec((1, span, chans), lambda i, m: (i // per_round, 0, 0)),
            pl.BlockSpec((chans, width), lambda i, m: (0, 0)),
        ],
        out_specs=[
            pl.BlockSpec((1, GROUP, lag_count), lambda i, m: (i, 0, 0)),
            pl.BlockSpec((1, GROUP, 128), lambda i, m: (i, 0, 0)),
        ],
    )
    corr, power = pl.pallas_call(
        correlate_kernel,
        grid_spec=grid_spec,
        out_shape=[
            jax.ShapeDtypeStruct((steps, GROUP, lag_count), jnp.float32),
            jax.ShapeDtypeStruct((steps, GROUP, 128), jnp.float32),
        ],
        cost_estimate=cost,
    )(meta, blocks, extended)
    return corr.reshape(rounds * count, lag_count), power[:, :, 0].reshape(rounds * count)


def window_sum(values, taps, lag_count):
    span = 1
    while span < taps:
        values = values[:, :-span] + values[:, span:]
        span *= 2
    return values[:, :lag_count]


def shards(signal, round_shard, offsets, chan_range):
    chan_local, lag_count = signal.shape
    rounds, count = offsets.shape
    section = lax.axis_index("sec")
    place = lax.axis_index("tm")
    total_lags = lag_count * lax.axis_size("tm")

    right_rim = from_behind(signal[:, :L], "tm", -1)
    extended = jnp.concatenate([signal, right_rim], axis=1)
    channel = section * chan_local + jnp.arange(chan_local, dtype=jnp.int32)
    lower = chan_range[:, :, 0]
    upper = chan_range[:, :, 1]
    inside = (channel >= lower[:, :, None]) & (channel < upper[:, :, None])

    flipped = jnp.transpose(signal)
    own = place == round_shard
    blocks = jnp.where(own[:, None, None], flipped[None], jnp.zeros_like(flipped)[None])
    blocks = lax.psum(blocks, "tm")
    offs = jnp.clip(offsets, 0, lag_count - L)
    first = jnp.minimum((offs // 16) * 16, lag_count - REACH)
    base = section * chan_local
    meta = jnp.stack([first, offs - first, lower - base, upper - base], axis=-1).reshape(-1)

    squares = jnp.square(extended.astype(jnp.float32))
    high = lax.reduce_precision(squares, exponent_bits=8, mantissa_bits=7)
    low = (squares - high).astype(jnp.bfloat16)
    masks = inside.reshape(rounds * count, chan_local).astype(jnp.bfloat16)
    summed = jnp.dot(masks, high.astype(jnp.bfloat16), preferred_element_type=jnp.float32)
    summed = summed + jnp.dot(masks, low, preferred_element_type=jnp.float32)
    energy_local = window_sum(summed, L, lag_count)

    corr_local, local_power = correlate(meta.astype(jnp.int32), blocks, extended, count)
    tmpl_power = group_sum(local_power, "sec")
    both = group_sum(jnp.stack([corr_local, energy_local]), "sec")
    corr, energy = both[0], both[1]
    normed = corr / jnp.sqrt(energy * tmpl_power[:, None] + EPS)
    power_sum = group_sum(jnp.sum(normed * normed, axis=1), "tm")
    meansq = power_sum / total_lags
    scored = normed / jnp.sqrt(meansq[:, None] + EPS)
    return scored.reshape(rounds, count, lag_count)


def solution(mesh):
    placed = (P("sec", "tm"), P(), P(), P())
    return jax.shard_map(
        shards, mesh=mesh, in_specs=placed, out_specs=P(None, None, "tm"), check_vma=False
    )
```

```python
import jax
import jax.numpy as jnp
from jax import lax
from jax.experimental import pallas as pl
from jax.experimental.pallas import tpu as pltpu
from jax.sharding import PartitionSpec as P

L = 128
GROUP = 4
REACH = L + 16

EPS = 1e-06


def from_behind(value, axis, by):
    length = lax.axis_size(axis)
    pairs = [(i, i + by) for i in range(length) if 0 <= i + by < length]
    return lax.ppermute(value, axis, pairs)


def group_sum(value, axis):
    size = lax.axis_size(axis)
    place = lax.axis_index(axis)
    stride = 1
    while stride < size:
        fan = 4 if size % (stride * 4) == 0 else 2 if size % (stride * 2) == 0 else 0
        if fan == 0:
            return lax.psum(value, axis)
        member = (place // stride) % fan
        got = {0: value}
        for d in range(1, fan):
            pairs = [(i, i ^ (d * stride)) for i in range(size)]
            got[d] = lax.ppermute(value, axis, pairs)
        total = None
        for m in range(fan):
            part = got[0]
            for d in range(1, fan):
                part = jnp.where((member ^ d) == m, got[d], part)
            total = part if total is None else total + part
        value = total
        stride *= fan
    return value


def spread_blocks(block, roots, axis):
    size = lax.axis_size(axis)
    place = lax.axis_index(axis)
    nbits = size.bit_length() - 1
    rounds = roots.shape[0]
    rows, chans = block.shape
    parts = next(p for p in (4, 2, 1) if rows % (p * size) == 0)
    if size & (size - 1) or rows % (parts * size) or nbits == 0:
        own = place == roots
        masked = jnp.where(own[:, None, None], block[None], jnp.zeros_like(block)[None])
        return lax.psum(masked, axis)
    piece = rows // (parts * size)
    orders = [[1 << ((p + s) % nbits) for s in range(nbits)] for p in range(parts)]
    bufs = {}
    for p in range(parts):
        seg = block[p * piece * size : (p + 1) * piece * size].reshape([2] * nbits + [piece, chans])
        perm = [nbits - 1 - (m.bit_length() - 1) for m in orders[p]] + [nbits, nbits + 1]
        seg = jnp.transpose(seg, perm)
        for r in range(rounds):
            bufs[p, r] = seg
    for s in range(nbits):
        sends, keeps = {}, {}
        for (p, r), buf in bufs.items():
            mask = orders[p][s]
            bit = (place // mask) % 2
            keeps[p, r] = jnp.where(bit == 1, buf[1], buf[0])
            sends.setdefault(mask, []).append(((p, r), jnp.where(bit == 1, buf[0], buf[1])))
        for mask, items in sends.items():
            got = lax.ppermute(jnp.stack([v for _, v in items]), axis, [(i, i ^ mask) for i in range(size)])
            for n, (key, _) in enumerate(items):
                held = sum(orders[key[0]][:s])
                holder = ((place ^ roots[key[1]]) & (size - 1 - held)) == 0
                bufs[key] = jnp.where(holder, keeps[key], got[n])
    for s in reversed(range(nbits)):
        sends = {}
        for (p, r), buf in bufs.items():
            sends.setdefault(orders[p][s], []).append(((p, r), buf))
        for mask, items in sends.items():
            got = lax.ppermute(jnp.stack([v for _, v in items]), axis, [(i, i ^ mask) for i in range(size)])
            bit = (place // mask) % 2
            for n, (key, buf) in enumerate(items):
                low = jnp.where(bit == 1, got[n], buf)
                high = jnp.where(bit == 1, buf, got[n])
                bufs[key] = jnp.stack([low, high])
    out = []
    for r in range(rounds):
        segs = []
        for p in range(parts):
            perm = [nbits - 1 - (m.bit_length() - 1) for m in orders[p]]
            inverse = [perm.index(k) for k in range(nbits)] + [nbits, nbits + 1]
            segs.append(jnp.transpose(bufs[p, r], inverse).reshape(piece * size, chans))
        out.append(jnp.concatenate(segs, axis=0))
    return jnp.stack(out)


def correlate_kernel(meta_ref, blk_ref, ext_ref, corr_ref, power_ref):
    step = pl.program_id(0)
    chans = blk_ref.shape[2]
    width = ext_ref.shape[1]
    group = corr_ref.shape[1]
    lags = corr_ref.shape[2]
    tap = lax.broadcasted_iota(jnp.int32, (L, REACH), 0)
    col = lax.broadcasted_iota(jnp.int32, (L, REACH), 1)
    lane = lax.broadcasted_iota(jnp.int32, (L, chans), 1)
    pieces = []
    for g in range(group):
        idx = step * group + g
        first = meta_ref[4 * idx]
        shift = meta_ref[4 * idx + 1]
        lower = meta_ref[4 * idx + 2]
        upper = meta_ref[4 * idx + 3]
        rows = blk_ref[0, pl.ds(pl.multiple_of(first, 16), REACH), :]
        pick = (col == shift + (L - 1) - tap).astype(jnp.bfloat16)
        chosen = jnp.dot(pick, rows, preferred_element_type=jnp.float32)
        chosen = jnp.where((lane >= lower) & (lane < upper), chosen, 0.0)
        power_ref[0, g : g + 1, :] = jnp.full((1, 128), jnp.sum(chosen * chosen), jnp.float32)
        pieces.append(chosen.astype(jnp.bfloat16))
    product = jnp.dot(
        jnp.concatenate(pieces, axis=0), ext_ref[...], preferred_element_type=jnp.float32
    )
    for g in range(group):
        rows = product[g * L : (g + 1) * L]
        sheared = pltpu.roll(rows, width - (L - 1), 1, stride=1, stride_axis=0)
        corr_ref[0, g : g + 1, :] = jnp.sum(sheared, axis=0, keepdims=True)[:, :lags]


def correlate(meta, blocks, extended, count):
    rounds, span, chans = blocks.shape
    width = extended.shape[1]
    lag_count = span
    steps = rounds * count // GROUP
    per_round = count // GROUP
    cost = pl.CostEstimate(
        flops=2 * rounds * count * L * (chans * width + REACH * chans),
        transcendentals=0,
        bytes_accessed=blocks.size * 2 + extended.size * 2 + rounds * count * lag_count * 4,
    )
    grid_spec = pltpu.PrefetchScalarGridSpec(
        num_scalar_prefetch=1,
        grid=(steps,),
        in_specs=[
            pl.BlockSpec((1, span, chans), lambda i, m: (i // per_round, 0, 0)),
            pl.BlockSpec((chans, width), lambda i, m: (0, 0)),
        ],
        out_specs=[
            pl.BlockSpec((1, GROUP, lag_count), lambda i, m: (i, 0, 0)),
            pl.BlockSpec((1, GROUP, 128), lambda i, m: (i, 0, 0)),
        ],
    )
    corr, power = pl.pallas_call(
        correlate_kernel,
        grid_spec=grid_spec,
        out_shape=[
            jax.ShapeDtypeStruct((steps, GROUP, lag_count), jnp.float32),
            jax.ShapeDtypeStruct((steps, GROUP, 128), jnp.float32),
        ],
        cost_estimate=cost,
    )(meta, blocks, extended)
    return corr.reshape(rounds * count, lag_count), power[:, :, 0].reshape(rounds * count)


def window_sum(values, taps, lag_count):
    span = 1
    while span < taps:
        values = values[:, :-span] + values[:, span:]
        span *= 2
    return values[:, :lag_count]


def shards(signal, round_shard, offsets, chan_range):
    chan_local, lag_count = signal.shape
    rounds, count = offsets.shape
    section = lax.axis_index("sec")
    place = lax.axis_index("tm")
    total_lags = lag_count * lax.axis_size("tm")

    right_rim = from_behind(signal[:, :L], "tm", -1)
    extended = jnp.concatenate([signal, right_rim], axis=1)
    channel = section * chan_local + jnp.arange(chan_local, dtype=jnp.int32)
    lower = chan_range[:, :, 0]
    upper = chan_range[:, :, 1]
    inside = (channel >= lower[:, :, None]) & (channel < upper[:, :, None])

    blocks = spread_blocks(jnp.transpose(signal), round_shard, "tm")
    offs = jnp.clip(offsets, 0, lag_count - L)
    first = jnp.minimum((offs // 16) * 16, lag_count - REACH)
    base = section * chan_local
    meta = jnp.stack([first, offs - first, lower - base, upper - base], axis=-1).reshape(-1)

    squares = jnp.square(extended.astype(jnp.float32))
    high = lax.reduce_precision(squares, exponent_bits=8, mantissa_bits=7)
    low = (squares - high).astype(jnp.bfloat16)
    masks = inside.reshape(rounds * count, chan_local).astype(jnp.bfloat16)
    summed = jnp.dot(masks, high.astype(jnp.bfloat16), preferred_element_type=jnp.float32)
    summed = summed + jnp.dot(masks, low, preferred_element_type=jnp.float32)
    energy_local = window_sum(summed, L, lag_count)

    corr_local, local_power = correlate(meta.astype(jnp.int32), blocks, extended, count)
    tmpl_power = group_sum(local_power, "sec")
    both = group_sum(jnp.stack([corr_local, energy_local]), "sec")
    corr, energy = both[0], both[1]
    normed = corr / jnp.sqrt(energy * tmpl_power[:, None] + EPS)
    power_sum = group_sum(jnp.sum(normed * normed, axis=1), "tm")
    meansq = power_sum / total_lags
    scored = normed / jnp.sqrt(meansq[:, None] + EPS)
    return scored.reshape(rounds, count, lag_count)


def solution(mesh):
    placed = (P("sec", "tm"), P(), P(), P())
    return jax.shard_map(
        shards, mesh=mesh, in_specs=placed, out_specs=P(None, None, "tm"), check_vma=False
    )
```

```python
import jax
import jax.numpy as jnp
from jax import lax
from jax.experimental import pallas as pl
from jax.experimental.pallas import tpu as pltpu
from jax.sharding import PartitionSpec as P

L = 128
GROUP = 8
REACH = L + 16

EPS = 1e-06


def from_behind(value, axis, by):
    length = lax.axis_size(axis)
    pairs = [(i, i + by) for i in range(length) if 0 <= i + by < length]
    return lax.ppermute(value, axis, pairs)


def group_sum(value, axis):
    size = lax.axis_size(axis)
    place = lax.axis_index(axis)
    stride = 1
    while stride < size:
        fan = 4 if size % (stride * 4) == 0 else 2 if size % (stride * 2) == 0 else 0
        if fan == 0:
            return lax.psum(value, axis)
        member = (place // stride) % fan
        got = {0: value}
        for d in range(1, fan):
            pairs = [(i, i ^ (d * stride)) for i in range(size)]
            got[d] = lax.ppermute(value, axis, pairs)
        total = None
        for m in range(fan):
            part = got[0]
            for d in range(1, fan):
                part = jnp.where((member ^ d) == m, got[d], part)
            total = part if total is None else total + part
        value = total
        stride *= fan
    return value


def spread_blocks(block, roots, axis):
    size = lax.axis_size(axis)
    place = lax.axis_index(axis)
    nbits = size.bit_length() - 1
    rounds = roots.shape[0]
    rows, chans = block.shape
    parts = next(p for p in (2, 1) if rows % (p * size) == 0)
    if size & (size - 1) or rows % (parts * size) or nbits == 0:
        own = place == roots
        masked = jnp.where(own[:, None, None], block[None], jnp.zeros_like(block)[None])
        return lax.psum(masked, axis)
    piece = rows // (parts * size)
    orders = {}
    for r in range(rounds):
        for p in range(parts):
            order = [1 << ((p * nbits // parts + s) % nbits) for s in range(nbits)]
            if r % 2:
                order = [order[s ^ 1] if (s ^ 1) < nbits else order[s] for s in range(nbits)]
            orders[p, r] = order
    bufs = {}
    for (p, r), order in orders.items():
        seg = block[p * piece * size : (p + 1) * piece * size].reshape([2] * nbits + [piece, chans])
        perm = [nbits - 1 - (m.bit_length() - 1) for m in order] + [nbits, nbits + 1]
        bufs[p, r] = jnp.transpose(seg, perm)
    for s in range(nbits):
        sends, keeps = {}, {}
        for (p, r), buf in bufs.items():
            mask = orders[p, r][s]
            bit = (place // mask) % 2
            keeps[p, r] = jnp.where(bit == 1, buf[1], buf[0])
            sends.setdefault(mask, []).append(((p, r), jnp.where(bit == 1, buf[0], buf[1])))
        for mask, items in sends.items():
            got = lax.ppermute(jnp.stack([v for _, v in items]), axis, [(i, i ^ mask) for i in range(size)])
            for n, (key, _) in enumerate(items):
                held = sum(orders[key][:s])
                holder = ((place ^ roots[key[1]]) & (size - 1 - held)) == 0
                bufs[key] = jnp.where(holder, keeps[key], got[n])
    for s in reversed(range(nbits)):
        sends = {}
        for (p, r), buf in bufs.items():
            sends.setdefault(orders[p, r][s], []).append(((p, r), buf))
        for mask, items in sends.items():
            got = lax.ppermute(jnp.stack([v for _, v in items]), axis, [(i, i ^ mask) for i in range(size)])
            bit = (place // mask) % 2
            for n, (key, buf) in enumerate(items):
                low = jnp.where(bit == 1, got[n], buf)
                high = jnp.where(bit == 1, buf, got[n])
                bufs[key] = jnp.stack([low, high])
    out = []
    for r in range(rounds):
        segs = []
        for p in range(parts):
            perm = [nbits - 1 - (m.bit_length() - 1) for m in orders[p, r]]
            inverse = [perm.index(k) for k in range(nbits)] + [nbits, nbits + 1]
            segs.append(jnp.transpose(bufs[p, r], inverse).reshape(piece * size, chans))
        out.append(jnp.concatenate(segs, axis=0))
    return jnp.stack(out)


def correlate_kernel(meta_ref, blk_ref, ext_ref, corr_ref, power_ref):
    step = pl.program_id(0)
    chans = blk_ref.shape[2]
    width = ext_ref.shape[1]
    group = corr_ref.shape[1]
    lags = corr_ref.shape[2]
    tap = lax.broadcasted_iota(jnp.int32, (L, REACH), 0)
    col = lax.broadcasted_iota(jnp.int32, (L, REACH), 1)
    lane = lax.broadcasted_iota(jnp.int32, (L, chans), 1)
    pieces = []
    for g in range(group):
        idx = step * group + g
        first = meta_ref[4 * idx]
        shift = meta_ref[4 * idx + 1]
        lower = meta_ref[4 * idx + 2]
        upper = meta_ref[4 * idx + 3]
        rows = blk_ref[0, pl.ds(pl.multiple_of(first, 16), REACH), :]
        pick = (col == shift + (L - 1) - tap).astype(jnp.bfloat16)
        chosen = jnp.dot(pick, rows, preferred_element_type=jnp.float32)
        chosen = jnp.where((lane >= lower) & (lane < upper), chosen, 0.0)
        power_ref[0, g : g + 1, :] = jnp.full((1, 128), jnp.sum(chosen * chosen), jnp.float32)
        pieces.append(chosen.astype(jnp.bfloat16))
    product = jnp.dot(
        jnp.concatenate(pieces, axis=0), ext_ref[...], preferred_element_type=jnp.float32
    )
    for g in range(group):
        rows = product[g * L : (g + 1) * L]
        sheared = pltpu.roll(rows, width - (L - 1), 1, stride=1, stride_axis=0)
        corr_ref[0, g : g + 1, :] = jnp.sum(sheared, axis=0, keepdims=True)[:, :lags]


def correlate(meta, blocks, extended, count):
    rounds, span, chans = blocks.shape
    width = extended.shape[1]
    lag_count = span
    steps = rounds * count // GROUP
    per_round = count // GROUP
    cost = pl.CostEstimate(
        flops=2 * rounds * count * L * (chans * width + REACH * chans),
        transcendentals=0,
        bytes_accessed=blocks.size * 2 + extended.size * 2 + rounds * count * lag_count * 4,
    )
    grid_spec = pltpu.PrefetchScalarGridSpec(
        num_scalar_prefetch=1,
        grid=(steps,),
        in_specs=[
            pl.BlockSpec((1, span, chans), lambda i, m: (i // per_round, 0, 0)),
            pl.BlockSpec((chans, width), lambda i, m: (0, 0)),
        ],
        out_specs=[
            pl.BlockSpec((1, GROUP, lag_count), lambda i, m: (i, 0, 0)),
            pl.BlockSpec((1, GROUP, 128), lambda i, m: (i, 0, 0)),
        ],
    )
    corr, power = pl.pallas_call(
        correlate_kernel,
        grid_spec=grid_spec,
        out_shape=[
            jax.ShapeDtypeStruct((steps, GROUP, lag_count), jnp.float32),
            jax.ShapeDtypeStruct((steps, GROUP, 128), jnp.float32),
        ],
        cost_estimate=cost,
    )(meta, blocks, extended)
    return corr.reshape(rounds * count, lag_count), power[:, :, 0].reshape(rounds * count)


def window_sum(values, taps, lag_count):
    span = 1
    while span < taps:
        values = values[:, :-span] + values[:, span:]
        span *= 2
    return values[:, :lag_count]


def shards(signal, round_shard, offsets, chan_range):
    chan_local, lag_count = signal.shape
    rounds, count = offsets.shape
    section = lax.axis_index("sec")
    place = lax.axis_index("tm")
    total_lags = lag_count * lax.axis_size("tm")

    right_rim = from_behind(signal[:, :L], "tm", -1)
    extended = jnp.concatenate([signal, right_rim], axis=1)
    channel = section * chan_local + jnp.arange(chan_local, dtype=jnp.int32)
    lower = chan_range[:, :, 0]
    upper = chan_range[:, :, 1]
    inside = (channel >= lower[:, :, None]) & (channel < upper[:, :, None])

    blocks = spread_blocks(jnp.transpose(signal), round_shard, "tm")
    offs = jnp.clip(offsets, 0, lag_count - L)
    first = jnp.minimum((offs // 16) * 16, lag_count - REACH)
    base = section * chan_local
    meta = jnp.stack([first, offs - first, lower - base, upper - base], axis=-1).reshape(-1)

    squares = jnp.square(extended.astype(jnp.float32))
    high = lax.reduce_precision(squares, exponent_bits=8, mantissa_bits=7)
    low = (squares - high).astype(jnp.bfloat16)
    masks = inside.reshape(rounds * count, chan_local).astype(jnp.bfloat16)
    summed = jnp.dot(masks, high.astype(jnp.bfloat16), preferred_element_type=jnp.float32)
    summed = summed + jnp.dot(masks, low, preferred_element_type=jnp.float32)
    energy_local = window_sum(summed, L, lag_count)

    corr_local, local_power = correlate(meta.astype(jnp.int32), blocks, extended, count)
    tmpl_power = group_sum(local_power, "sec")
    both = group_sum(jnp.stack([corr_local, energy_local]), "sec")
    corr, energy = both[0], both[1]
    normed = corr / jnp.sqrt(energy * tmpl_power[:, None] + EPS)
    power_sum = group_sum(jnp.sum(normed * normed, axis=1), "tm")
    meansq = power_sum / total_lags
    scored = normed / jnp.sqrt(meansq[:, None] + EPS)
    return scored.reshape(rounds, count, lag_count)


def solution(mesh):
    placed = (P("sec", "tm"), P(), P(), P())
    return jax.shard_map(
        shards, mesh=mesh, in_specs=placed, out_specs=P(None, None, "tm"), check_vma=False
    )
```

```python
import jax
import jax.numpy as jnp
from jax import lax
from jax.experimental import pallas as pl
from jax.experimental.pallas import tpu as pltpu
from jax.sharding import PartitionSpec as P

L = 128
GROUP = 4
CHUNK = 256
REACH = L + 16

EPS = 1e-06


def from_behind(value, axis, by):
    length = lax.axis_size(axis)
    pairs = [(i, i + by) for i in range(length) if 0 <= i + by < length]
    return lax.ppermute(value, axis, pairs)


def group_sum(value, axis):
    size = lax.axis_size(axis)
    place = lax.axis_index(axis)
    stride = 1
    while stride < size:
        fan = 4 if size % (stride * 4) == 0 else 2 if size % (stride * 2) == 0 else 0
        if fan == 0:
            return lax.psum(value, axis)
        member = (place // stride) % fan
        got = {0: value}
        for d in range(1, fan):
            pairs = [(i, i ^ (d * stride)) for i in range(size)]
            got[d] = lax.ppermute(value, axis, pairs)
        total = None
        for m in range(fan):
            part = got[0]
            for d in range(1, fan):
                part = jnp.where((member ^ d) == m, got[d], part)
            total = part if total is None else total + part
        value = total
        stride *= fan
    return value


def spread_blocks(block, roots, axis):
    size = lax.axis_size(axis)
    place = lax.axis_index(axis)
    nbits = size.bit_length() - 1
    rounds = roots.shape[0]
    rows, chans = block.shape
    parts = next(p for p in (2, 1) if rows % (p * size) == 0)
    if size & (size - 1) or rows % (parts * size) or nbits == 0:
        own = place == roots
        masked = jnp.where(own[:, None, None], block[None], jnp.zeros_like(block)[None])
        return lax.psum(masked, axis)
    piece = rows // (parts * size)
    orders = {}
    for r in range(rounds):
        for p in range(parts):
            order = [1 << ((p * nbits // parts + s) % nbits) for s in range(nbits)]
            if r % 2:
                order = [order[s ^ 1] if (s ^ 1) < nbits else order[s] for s in range(nbits)]
            orders[p, r] = order
    bufs = {}
    for (p, r), order in orders.items():
        seg = block[p * piece * size : (p + 1) * piece * size].reshape([2] * nbits + [piece, chans])
        perm = [nbits - 1 - (m.bit_length() - 1) for m in order] + [nbits, nbits + 1]
        bufs[p, r] = jnp.transpose(seg, perm)
    for s in range(nbits):
        sends, keeps = {}, {}
        for (p, r), buf in bufs.items():
            mask = orders[p, r][s]
            bit = (place // mask) % 2
            keeps[p, r] = jnp.where(bit == 1, buf[1], buf[0])
            sends.setdefault(mask, []).append(((p, r), jnp.where(bit == 1, buf[0], buf[1])))
        for mask, items in sends.items():
            got = lax.ppermute(jnp.stack([v for _, v in items]), axis, [(i, i ^ mask) for i in range(size)])
            for n, (key, _) in enumerate(items):
                held = sum(orders[key][:s])
                holder = ((place ^ roots[key[1]]) & (size - 1 - held)) == 0
                bufs[key] = jnp.where(holder, keeps[key], got[n])
    for s in reversed(range(nbits)):
        sends = {}
        for (p, r), buf in bufs.items():
            sends.setdefault(orders[p, r][s], []).append(((p, r), buf))
        for mask, items in sends.items():
            got = lax.ppermute(jnp.stack([v for _, v in items]), axis, [(i, i ^ mask) for i in range(size)])
            bit = (place // mask) % 2
            for n, (key, buf) in enumerate(items):
                low = jnp.where(bit == 1, got[n], buf)
                high = jnp.where(bit == 1, buf, got[n])
                bufs[key] = jnp.stack([low, high])
    out = []
    for r in range(rounds):
        segs = []
        for p in range(parts):
            perm = [nbits - 1 - (m.bit_length() - 1) for m in orders[p, r]]
            inverse = [perm.index(k) for k in range(nbits)] + [nbits, nbits + 1]
            segs.append(jnp.transpose(bufs[p, r], inverse).reshape(piece * size, chans))
        out.append(jnp.concatenate(segs, axis=0))
    return jnp.stack(out)


def correlate_kernel(meta_ref, blk_ref, ext_ref, corr_ref, power_ref, tmpl_ref, acc_ref):
    step = pl.program_id(0)
    chans = blk_ref.shape[2]
    width = ext_ref.shape[1]
    group = corr_ref.shape[1]
    lags = corr_ref.shape[2]
    tap = lax.broadcasted_iota(jnp.int32, (L, REACH), 0)
    col = lax.broadcasted_iota(jnp.int32, (L, REACH), 1)
    lane = lax.broadcasted_iota(jnp.int32, (L, chans), 1)
    for g in range(group):
        idx = step * group + g
        first = meta_ref[4 * idx]
        shift = meta_ref[4 * idx + 1]
        lower = meta_ref[4 * idx + 2]
        upper = meta_ref[4 * idx + 3]
        rows = blk_ref[0, pl.ds(pl.multiple_of(first, 16), REACH), :]
        pick = (col == shift + (L - 1) - tap).astype(jnp.bfloat16)
        chosen = jnp.dot(pick, rows, preferred_element_type=jnp.float32)
        chosen = jnp.where((lane >= lower) & (lane < upper), chosen, 0.0)
        power_ref[0, g : g + 1, :] = jnp.full((1, 128), jnp.sum(chosen * chosen), jnp.float32)
        tmpl_ref[...] = chosen.astype(jnp.bfloat16)
        acc_ref[...] = jnp.zeros_like(acc_ref)
        for q in range(chans // CHUNK):
            @pl.when((q * CHUNK < upper) & ((q + 1) * CHUNK > lower))
            def _():
                acc_ref[...] += jnp.dot(
                    tmpl_ref[:, q * CHUNK : (q + 1) * CHUNK],
                    ext_ref[q * CHUNK : (q + 1) * CHUNK, :],
                    preferred_element_type=jnp.float32,
                )
        sheared = pltpu.roll(acc_ref[...], width - (L - 1), 1, stride=1, stride_axis=0)
        corr_ref[0, g : g + 1, :] = jnp.sum(sheared, axis=0, keepdims=True)[:, :lags]


def correlate(meta, blocks, extended, count):
    rounds, span, chans = blocks.shape
    width = extended.shape[1]
    lag_count = span
    steps = rounds * count // GROUP
    per_round = count // GROUP
    cost = pl.CostEstimate(
        flops=2 * rounds * count * L * (chans * width + REACH * chans),
        transcendentals=0,
        bytes_accessed=blocks.size * 2 + extended.size * 2 + rounds * count * lag_count * 4,
    )
    grid_spec = pltpu.PrefetchScalarGridSpec(
        num_scalar_prefetch=1,
        grid=(steps,),
        in_specs=[
            pl.BlockSpec((1, span, chans), lambda i, m: (i // per_round, 0, 0)),
            pl.BlockSpec((chans, width), lambda i, m: (0, 0)),
        ],
        out_specs=[
            pl.BlockSpec((1, GROUP, lag_count), lambda i, m: (i, 0, 0)),
            pl.BlockSpec((1, GROUP, 128), lambda i, m: (i, 0, 0)),
        ],
        scratch_shapes=[pltpu.VMEM((L, chans), jnp.bfloat16), pltpu.VMEM((L, width), jnp.float32)],
    )
    corr, power = pl.pallas_call(
        correlate_kernel,
        grid_spec=grid_spec,
        out_shape=[
            jax.ShapeDtypeStruct((steps, GROUP, lag_count), jnp.float32),
            jax.ShapeDtypeStruct((steps, GROUP, 128), jnp.float32),
        ],
        cost_estimate=cost,
    )(meta, blocks, extended)
    return corr.reshape(rounds * count, lag_count), power[:, :, 0].reshape(rounds * count)


def window_sum(values, taps, lag_count):
    span = 1
    while span < taps:
        values = values[:, :-span] + values[:, span:]
        span *= 2
    return values[:, :lag_count]


def shards(signal, round_shard, offsets, chan_range):
    chan_local, lag_count = signal.shape
    rounds, count = offsets.shape
    section = lax.axis_index("sec")
    place = lax.axis_index("tm")
    total_lags = lag_count * lax.axis_size("tm")

    right_rim = from_behind(signal[:, :L], "tm", -1)
    extended = jnp.concatenate([signal, right_rim], axis=1)
    channel = section * chan_local + jnp.arange(chan_local, dtype=jnp.int32)
    lower = chan_range[:, :, 0]
    upper = chan_range[:, :, 1]
    inside = (channel >= lower[:, :, None]) & (channel < upper[:, :, None])

    blocks = spread_blocks(jnp.transpose(signal), round_shard, "tm")
    offs = jnp.clip(offsets, 0, lag_count - L)
    first = jnp.minimum((offs // 16) * 16, lag_count - REACH)
    base = section * chan_local
    meta = jnp.stack([first, offs - first, lower - base, upper - base], axis=-1).reshape(-1)

    squares = jnp.square(extended.astype(jnp.float32))
    high = lax.reduce_precision(squares, exponent_bits=8, mantissa_bits=7)
    low = (squares - high).astype(jnp.bfloat16)
    masks = inside.reshape(rounds * count, chan_local).astype(jnp.bfloat16)
    summed = jnp.dot(masks, high.astype(jnp.bfloat16), preferred_element_type=jnp.float32)
    summed = summed + jnp.dot(masks, low, preferred_element_type=jnp.float32)
    energy_local = window_sum(summed, L, lag_count)

    corr_local, local_power = correlate(meta.astype(jnp.int32), blocks, extended, count)
    tmpl_power = group_sum(local_power, "sec")
    both = group_sum(jnp.stack([corr_local, energy_local]), "sec")
    corr, energy = both[0], both[1]
    normed = corr / jnp.sqrt(energy * tmpl_power[:, None] + EPS)
    power_sum = group_sum(jnp.sum(normed * normed, axis=1), "tm")
    meansq = power_sum / total_lags
    scored = normed / jnp.sqrt(meansq[:, None] + EPS)
    return scored.reshape(rounds, count, lag_count)


def solution(mesh):
    placed = (P("sec", "tm"), P(), P(), P())
    return jax.shard_map(
        shards, mesh=mesh, in_specs=placed, out_specs=P(None, None, "tm"), check_vma=False
    )
```

```python
import jax
import jax.numpy as jnp
from jax import lax
from jax.experimental import pallas as pl
from jax.experimental.pallas import tpu as pltpu
from jax.sharding import PartitionSpec as P

L = 128
GROUP = 4
REACH = L + 16

EPS = 1e-06


def from_behind(value, axis, by):
    length = lax.axis_size(axis)
    pairs = [(i, i + by) for i in range(length) if 0 <= i + by < length]
    return lax.ppermute(value, axis, pairs)


def group_sum(value, axis):
    size = lax.axis_size(axis)
    place = lax.axis_index(axis)
    stride = 1
    while stride < size:
        fan = 4 if size % (stride * 4) == 0 else 2 if size % (stride * 2) == 0 else 0
        if fan == 0:
            return lax.psum(value, axis)
        member = (place // stride) % fan
        got = {0: value}
        for d in range(1, fan):
            pairs = [(i, i ^ (d * stride)) for i in range(size)]
            got[d] = lax.ppermute(value, axis, pairs)
        total = None
        for m in range(fan):
            part = got[0]
            for d in range(1, fan):
                part = jnp.where((member ^ d) == m, got[d], part)
            total = part if total is None else total + part
        value = total
        stride *= fan
    return value


def spread_blocks(block, roots, axis):
    size = lax.axis_size(axis)
    place = lax.axis_index(axis)
    nbits = size.bit_length() - 1
    rounds = roots.shape[0]
    rows, chans = block.shape
    parts = next(p for p in (4, 2, 1) if rows % (p * size) == 0)
    if size & (size - 1) or rows % (parts * size) or nbits == 0:
        own = place == roots
        masked = jnp.where(own[:, None, None], block[None], jnp.zeros_like(block)[None])
        return lax.psum(masked, axis)
    piece = rows // (parts * size)
    orders = [[1 << ((p + s) % nbits) for s in range(nbits)] for p in range(parts)]
    bufs = {}
    for p in range(parts):
        seg = block[p * piece * size : (p + 1) * piece * size].reshape([2] * nbits + [piece, chans])
        perm = [nbits - 1 - (m.bit_length() - 1) for m in orders[p]] + [nbits, nbits + 1]
        seg = jnp.transpose(seg, perm)
        for r in range(rounds):
            bufs[p, r] = seg
    for s in range(nbits):
        sends, keeps = {}, {}
        for (p, r), buf in bufs.items():
            mask = orders[p][s]
            bit = (place // mask) % 2
            keeps[p, r] = jnp.where(bit == 1, buf[1], buf[0])
            sends.setdefault(mask, []).append(((p, r), jnp.where(bit == 1, buf[0], buf[1])))
        for mask, items in sends.items():
            got = lax.ppermute(jnp.stack([v for _, v in items]), axis, [(i, i ^ mask) for i in range(size)])
            for n, (key, _) in enumerate(items):
                held = sum(orders[key[0]][:s])
                holder = ((place ^ roots[key[1]]) & (size - 1 - held)) == 0
                bufs[key] = jnp.where(holder, keeps[key], got[n])
    for s in reversed(range(nbits)):
        sends = {}
        for (p, r), buf in bufs.items():
            sends.setdefault((r if s == 0 else 0, orders[p][s]), []).append(((p, r), buf))
        for (_, mask), items in sorted(sends.items()):
            got = lax.ppermute(jnp.stack([v for _, v in items]), axis, [(i, i ^ mask) for i in range(size)])
            bit = (place // mask) % 2
            for n, (key, buf) in enumerate(items):
                low = jnp.where(bit == 1, got[n], buf)
                high = jnp.where(bit == 1, buf, got[n])
                bufs[key] = jnp.stack([low, high])
    out = []
    for r in range(rounds):
        segs = []
        for p in range(parts):
            perm = [nbits - 1 - (m.bit_length() - 1) for m in orders[p]]
            inverse = [perm.index(k) for k in range(nbits)] + [nbits, nbits + 1]
            segs.append(jnp.transpose(bufs[p, r], inverse).reshape(piece * size, chans))
        out.append(jnp.concatenate(segs, axis=0))
    return jnp.stack(out)


def correlate_kernel(meta_ref, blk_ref, ext_ref, corr_ref, power_ref):
    step = pl.program_id(0)
    chans = blk_ref.shape[2]
    width = ext_ref.shape[1]
    group = corr_ref.shape[1]
    lags = corr_ref.shape[2]
    tap = lax.broadcasted_iota(jnp.int32, (L, REACH), 0)
    col = lax.broadcasted_iota(jnp.int32, (L, REACH), 1)
    lane = lax.broadcasted_iota(jnp.int32, (L, chans), 1)
    pieces = []
    for g in range(group):
        idx = step * group + g
        first = meta_ref[4 * idx]
        shift = meta_ref[4 * idx + 1]
        lower = meta_ref[4 * idx + 2]
        upper = meta_ref[4 * idx + 3]
        rows = blk_ref[0, pl.ds(pl.multiple_of(first, 16), REACH), :]
        pick = (col == shift + (L - 1) - tap).astype(jnp.bfloat16)
        chosen = jnp.dot(pick, rows, preferred_element_type=jnp.float32)
        chosen = jnp.where((lane >= lower) & (lane < upper), chosen, 0.0)
        power_ref[0, g : g + 1, :] = jnp.full((1, 128), jnp.sum(chosen * chosen), jnp.float32)
        pieces.append(chosen.astype(jnp.bfloat16))
    product = jnp.dot(
        jnp.concatenate(pieces, axis=0), ext_ref[...], preferred_element_type=jnp.float32
    )
    for g in range(group):
        rows = product[g * L : (g + 1) * L]
        sheared = pltpu.roll(rows, width - (L - 1), 1, stride=1, stride_axis=0)
        corr_ref[0, g : g + 1, :] = jnp.sum(sheared, axis=0, keepdims=True)[:, :lags]


def correlate(meta, blocks, extended, count):
    rounds, span, chans = blocks.shape
    width = extended.shape[1]
    lag_count = span
    steps = rounds * count // GROUP
    per_round = count // GROUP
    cost = pl.CostEstimate(
        flops=2 * rounds * count * L * (chans * width + REACH * chans),
        transcendentals=0,
        bytes_accessed=blocks.size * 2 + extended.size * 2 + rounds * count * lag_count * 4,
    )
    grid_spec = pltpu.PrefetchScalarGridSpec(
        num_scalar_prefetch=1,
        grid=(steps,),
        in_specs=[
            pl.BlockSpec((1, span, chans), lambda i, m: (i // per_round, 0, 0)),
            pl.BlockSpec((chans, width), lambda i, m: (0, 0)),
        ],
        out_specs=[
            pl.BlockSpec((1, GROUP, lag_count), lambda i, m: (i, 0, 0)),
            pl.BlockSpec((1, GROUP, 128), lambda i, m: (i, 0, 0)),
        ],
    )
    corr, power = pl.pallas_call(
        correlate_kernel,
        grid_spec=grid_spec,
        out_shape=[
            jax.ShapeDtypeStruct((steps, GROUP, lag_count), jnp.float32),
            jax.ShapeDtypeStruct((steps, GROUP, 128), jnp.float32),
        ],
        cost_estimate=cost,
    )(meta, blocks, extended)
    return corr.reshape(rounds * count, lag_count), power[:, :, 0].reshape(rounds * count)


def window_sum(values, taps, lag_count):
    span = 1
    while span < taps:
        values = values[:, :-span] + values[:, span:]
        span *= 2
    return values[:, :lag_count]


def shards(signal, round_shard, offsets, chan_range):
    chan_local, lag_count = signal.shape
    rounds, count = offsets.shape
    section = lax.axis_index("sec")
    place = lax.axis_index("tm")
    total_lags = lag_count * lax.axis_size("tm")

    right_rim = from_behind(signal[:, :L], "tm", -1)
    extended = jnp.concatenate([signal, right_rim], axis=1)
    channel = section * chan_local + jnp.arange(chan_local, dtype=jnp.int32)
    lower = chan_range[:, :, 0]
    upper = chan_range[:, :, 1]
    inside = (channel >= lower[:, :, None]) & (channel < upper[:, :, None])

    blocks = spread_blocks(jnp.transpose(signal), round_shard, "tm")
    offs = jnp.clip(offsets, 0, lag_count - L)
    first = jnp.minimum((offs // 16) * 16, lag_count - REACH)
    base = section * chan_local
    meta = jnp.stack([first, offs - first, lower - base, upper - base], axis=-1).reshape(-1)

    squares = jnp.square(extended.astype(jnp.float32))
    high = lax.reduce_precision(squares, exponent_bits=8, mantissa_bits=7)
    low = (squares - high).astype(jnp.bfloat16)
    masks = inside.reshape(rounds * count, chan_local).astype(jnp.bfloat16)
    summed = jnp.dot(masks, high.astype(jnp.bfloat16), preferred_element_type=jnp.float32)
    summed = summed + jnp.dot(masks, low, preferred_element_type=jnp.float32)
    energy_local = window_sum(summed, L, lag_count)

    meta = meta.astype(jnp.int32).reshape(rounds, -1)
    pieces = [correlate(meta[r], blocks[r : r + 1], extended, count) for r in range(rounds)]
    corr_local = jnp.concatenate([c for c, _ in pieces])
    local_power = jnp.concatenate([p for _, p in pieces])
    tmpl_power = group_sum(local_power, "sec")
    both = group_sum(jnp.stack([corr_local, energy_local]), "sec")
    corr, energy = both[0], both[1]
    normed = corr / jnp.sqrt(energy * tmpl_power[:, None] + EPS)
    power_sum = group_sum(jnp.sum(normed * normed, axis=1), "tm")
    meansq = power_sum / total_lags
    scored = normed / jnp.sqrt(meansq[:, None] + EPS)
    return scored.reshape(rounds, count, lag_count)


def solution(mesh):
    placed = (P("sec", "tm"), P(), P(), P())
    return jax.shard_map(
        shards, mesh=mesh, in_specs=placed, out_specs=P(None, None, "tm"), check_vma=False
    )
```

```python
import jax
import jax.numpy as jnp
from jax import lax
from jax.experimental import pallas as pl
from jax.experimental.pallas import tpu as pltpu
from jax.sharding import PartitionSpec as P

L = 128
GROUP = 4
REACH = L + 16
SPLIT = 3

EPS = 1e-06


def from_behind(value, axis, by):
    length = lax.axis_size(axis)
    pairs = [(i, i + by) for i in range(length) if 0 <= i + by < length]
    return lax.ppermute(value, axis, pairs)


def group_sum(value, axis):
    size = lax.axis_size(axis)
    place = lax.axis_index(axis)
    stride = 1
    while stride < size:
        fan = 4 if size % (stride * 4) == 0 else 2 if size % (stride * 2) == 0 else 0
        if fan == 0:
            return lax.psum(value, axis)
        member = (place // stride) % fan
        got = {0: value}
        for d in range(1, fan):
            pairs = [(i, i ^ (d * stride)) for i in range(size)]
            got[d] = lax.ppermute(value, axis, pairs)
        total = None
        for m in range(fan):
            part = got[0]
            for d in range(1, fan):
                part = jnp.where((member ^ d) == m, got[d], part)
            total = part if total is None else total + part
        value = total
        stride *= fan
    return value


def spread_blocks(block, roots, axis):
    size = lax.axis_size(axis)
    place = lax.axis_index(axis)
    nbits = size.bit_length() - 1
    rounds = roots.shape[0]
    rows, chans = block.shape
    parts = next(p for p in (4, 2, 1) if rows % (p * size) == 0)
    if size & (size - 1) or rows % (parts * size) or nbits == 0:
        own = place == roots
        masked = jnp.where(own[:, None, None], block[None], jnp.zeros_like(block)[None])
        return lax.psum(masked, axis)
    piece = rows // (parts * size)
    orders = [[1 << ((p + s) % nbits) for s in range(nbits)] for p in range(parts)]
    bufs = {}
    for p in range(parts):
        seg = block[p * piece * size : (p + 1) * piece * size].reshape([2] * nbits + [piece, chans])
        perm = [nbits - 1 - (m.bit_length() - 1) for m in orders[p]] + [nbits, nbits + 1]
        seg = jnp.transpose(seg, perm)
        for r in range(rounds):
            bufs[p, r] = seg
    for s in range(nbits):
        sends, keeps = {}, {}
        for (p, r), buf in bufs.items():
            mask = orders[p][s]
            bit = (place // mask) % 2
            keeps[p, r] = jnp.where(bit == 1, buf[1], buf[0])
            sends.setdefault(mask, []).append(((p, r), jnp.where(bit == 1, buf[0], buf[1])))
        for mask, items in sends.items():
            got = lax.ppermute(jnp.stack([v for _, v in items]), axis, [(i, i ^ mask) for i in range(size)])
            for n, (key, _) in enumerate(items):
                held = sum(orders[key[0]][:s])
                holder = ((place ^ roots[key[1]]) & (size - 1 - held)) == 0
                bufs[key] = jnp.where(holder, keeps[key], got[n])
    for s in reversed(range(nbits)):
        sends = {}
        for (p, r), buf in bufs.items():
            sends.setdefault((r if s <= SPLIT else 0, orders[p][s]), []).append(((p, r), buf))
        for (_, mask), items in sorted(sends.items()):
            got = lax.ppermute(jnp.stack([v for _, v in items]), axis, [(i, i ^ mask) for i in range(size)])
            bit = (place // mask) % 2
            for n, (key, buf) in enumerate(items):
                low = jnp.where(bit == 1, got[n], buf)
                high = jnp.where(bit == 1, buf, got[n])
                bufs[key] = jnp.stack([low, high])
    out = []
    for r in range(rounds):
        segs = []
        for p in range(parts):
            perm = [nbits - 1 - (m.bit_length() - 1) for m in orders[p]]
            inverse = [perm.index(k) for k in range(nbits)] + [nbits, nbits + 1]
            segs.append(jnp.transpose(bufs[p, r], inverse).reshape(piece * size, chans))
        out.append(jnp.concatenate(segs, axis=0))
    return jnp.stack(out)


def correlate_kernel(meta_ref, blk_ref, ext_ref, corr_ref, power_ref):
    step = pl.program_id(0)
    chans = blk_ref.shape[2]
    width = ext_ref.shape[1]
    group = corr_ref.shape[1]
    lags = corr_ref.shape[2]
    tap = lax.broadcasted_iota(jnp.int32, (L, REACH), 0)
    col = lax.broadcasted_iota(jnp.int32, (L, REACH), 1)
    lane = lax.broadcasted_iota(jnp.int32, (L, chans), 1)
    pieces = []
    for g in range(group):
        idx = step * group + g
        first = meta_ref[4 * idx]
        shift = meta_ref[4 * idx + 1]
        lower = meta_ref[4 * idx + 2]
        upper = meta_ref[4 * idx + 3]
        rows = blk_ref[0, pl.ds(pl.multiple_of(first, 16), REACH), :]
        pick = (col == shift + (L - 1) - tap).astype(jnp.bfloat16)
        chosen = jnp.dot(pick, rows, preferred_element_type=jnp.float32)
        chosen = jnp.where((lane >= lower) & (lane < upper), chosen, 0.0)
        power_ref[0, g : g + 1, :] = jnp.full((1, 128), jnp.sum(chosen * chosen), jnp.float32)
        pieces.append(chosen.astype(jnp.bfloat16))
    product = jnp.dot(
        jnp.concatenate(pieces, axis=0), ext_ref[...], preferred_element_type=jnp.float32
    )
    for g in range(group):
        rows = product[g * L : (g + 1) * L]
        sheared = pltpu.roll(rows, width - (L - 1), 1, stride=1, stride_axis=0)
        corr_ref[0, g : g + 1, :] = jnp.sum(sheared, axis=0, keepdims=True)[:, :lags]


def correlate(meta, blocks, extended, count):
    rounds, span, chans = blocks.shape
    width = extended.shape[1]
    lag_count = span
    steps = rounds * count // GROUP
    per_round = count // GROUP
    cost = pl.CostEstimate(
        flops=2 * rounds * count * L * (chans * width + REACH * chans),
        transcendentals=0,
        bytes_accessed=blocks.size * 2 + extended.size * 2 + rounds * count * lag_count * 4,
    )
    grid_spec = pltpu.PrefetchScalarGridSpec(
        num_scalar_prefetch=1,
        grid=(steps,),
        in_specs=[
            pl.BlockSpec((1, span, chans), lambda i, m: (i // per_round, 0, 0)),
            pl.BlockSpec((chans, width), lambda i, m: (0, 0)),
        ],
        out_specs=[
            pl.BlockSpec((1, GROUP, lag_count), lambda i, m: (i, 0, 0)),
            pl.BlockSpec((1, GROUP, 128), lambda i, m: (i, 0, 0)),
        ],
    )
    corr, power = pl.pallas_call(
        correlate_kernel,
        grid_spec=grid_spec,
        out_shape=[
            jax.ShapeDtypeStruct((steps, GROUP, lag_count), jnp.float32),
            jax.ShapeDtypeStruct((steps, GROUP, 128), jnp.float32),
        ],
        cost_estimate=cost,
    )(meta, blocks, extended)
    return corr.reshape(rounds * count, lag_count), power[:, :, 0].reshape(rounds * count)


def window_sum(values, taps, lag_count):
    span = 1
    while span < taps:
        values = values[:, :-span] + values[:, span:]
        span *= 2
    return values[:, :lag_count]


def shards(signal, round_shard, offsets, chan_range):
    chan_local, lag_count = signal.shape
    rounds, count = offsets.shape
    section = lax.axis_index("sec")
    place = lax.axis_index("tm")
    total_lags = lag_count * lax.axis_size("tm")

    right_rim = from_behind(signal[:, :L], "tm", -1)
    extended = jnp.concatenate([signal, right_rim], axis=1)
    channel = section * chan_local + jnp.arange(chan_local, dtype=jnp.int32)
    lower = chan_range[:, :, 0]
    upper = chan_range[:, :, 1]
    inside = (channel >= lower[:, :, None]) & (channel < upper[:, :, None])

    blocks = spread_blocks(jnp.transpose(signal), round_shard, "tm")
    offs = jnp.clip(offsets, 0, lag_count - L)
    first = jnp.minimum((offs // 16) * 16, lag_count - REACH)
    base = section * chan_local
    meta = jnp.stack([first, offs - first, lower - base, upper - base], axis=-1).reshape(-1)

    squares = jnp.square(extended.astype(jnp.float32))
    high = lax.reduce_precision(squares, exponent_bits=8, mantissa_bits=7)
    low = (squares - high).astype(jnp.bfloat16)
    masks = inside.reshape(rounds * count, chan_local).astype(jnp.bfloat16)
    summed = jnp.dot(masks, high.astype(jnp.bfloat16), preferred_element_type=jnp.float32)
    summed = summed + jnp.dot(masks, low, preferred_element_type=jnp.float32)
    energy_local = window_sum(summed, L, lag_count)

    meta = meta.astype(jnp.int32).reshape(rounds, -1)
    pieces = [correlate(meta[r], blocks[r : r + 1], extended, count) for r in range(rounds)]
    corr_local = jnp.concatenate([c for c, _ in pieces])
    local_power = jnp.concatenate([p for _, p in pieces])
    tmpl_power = group_sum(local_power, "sec")
    both = group_sum(jnp.stack([corr_local, energy_local]), "sec")
    corr, energy = both[0], both[1]
    normed = corr / jnp.sqrt(energy * tmpl_power[:, None] + EPS)
    power_sum = group_sum(jnp.sum(normed * normed, axis=1), "tm")
    meansq = power_sum / total_lags
    scored = normed / jnp.sqrt(meansq[:, None] + EPS)
    return scored.reshape(rounds, count, lag_count)


def solution(mesh):
    placed = (P("sec", "tm"), P(), P(), P())
    return jax.shard_map(
        shards, mesh=mesh, in_specs=placed, out_specs=P(None, None, "tm"), check_vma=False
    )
```

```python
import jax
import jax.numpy as jnp
from jax import lax
from jax.experimental import pallas as pl
from jax.experimental.pallas import tpu as pltpu
from jax.sharding import PartitionSpec as P

L = 128
GROUP = 4
REACH = L + 16

EPS = 1e-06


def from_behind(value, axis, by):
    length = lax.axis_size(axis)
    pairs = [(i, i + by) for i in range(length) if 0 <= i + by < length]
    return lax.ppermute(value, axis, pairs)


def group_sum(value, axis):
    size = lax.axis_size(axis)
    place = lax.axis_index(axis)
    stride = 1
    while stride < size:
        fan = 4 if size % (stride * 4) == 0 else 2 if size % (stride * 2) == 0 else 0
        if fan == 0:
            return lax.psum(value, axis)
        member = (place // stride) % fan
        got = {0: value}
        for d in range(1, fan):
            pairs = [(i, i ^ (d * stride)) for i in range(size)]
            got[d] = lax.ppermute(value, axis, pairs)
        total = None
        for m in range(fan):
            part = got[0]
            for d in range(1, fan):
                part = jnp.where((member ^ d) == m, got[d], part)
            total = part if total is None else total + part
        value = total
        stride *= fan
    return value


def spread_blocks(block, roots, axis):
    size = lax.axis_size(axis)
    place = lax.axis_index(axis)
    nbits = size.bit_length() - 1
    rounds = roots.shape[0]
    rows, chans = block.shape
    parts = next(p for p in (4, 2, 1) if rows % (p * size) == 0)
    if size & (size - 1) or rows % (parts * size) or nbits == 0:
        own = place == roots
        masked = jnp.where(own[:, None, None], block[None], jnp.zeros_like(block)[None])
        return lax.psum(masked, axis)
    piece = rows // (parts * size)
    orders = [[1 << ((p + s) % nbits) for s in range(nbits)] for p in range(parts)]
    bufs = {}
    for p in range(parts):
        seg = block[p * piece * size : (p + 1) * piece * size].reshape([2] * nbits + [piece, chans])
        perm = [nbits - 1 - (m.bit_length() - 1) for m in orders[p]] + [nbits, nbits + 1]
        seg = jnp.transpose(seg, perm)
        for r in range(rounds):
            bufs[p, r] = seg
    for s in range(nbits):
        sends, keeps = {}, {}
        for (p, r), buf in bufs.items():
            mask = orders[p][s]
            bit = (place // mask) % 2
            keeps[p, r] = jnp.where(bit == 1, buf[1], buf[0])
            sends.setdefault(mask, []).append(((p, r), jnp.where(bit == 1, buf[0], buf[1])))
        for mask, items in sends.items():
            got = lax.ppermute(jnp.stack([v for _, v in items]), axis, [(i, i ^ mask) for i in range(size)])
            for n, (key, _) in enumerate(items):
                held = sum(orders[key[0]][:s])
                holder = ((place ^ roots[key[1]]) & (size - 1 - held)) == 0
                bufs[key] = jnp.where(holder, keeps[key], got[n])
    for s in reversed(range(nbits)):
        sends = {}
        for (p, r), buf in bufs.items():
            sends.setdefault((r if s == 0 else 0, orders[p][s]), []).append(((p, r), buf))
        for (_, mask), items in sorted(sends.items()):
            got = lax.ppermute(jnp.stack([v for _, v in items]), axis, [(i, i ^ mask) for i in range(size)])
            bit = (place // mask) % 2
            for n, (key, buf) in enumerate(items):
                low = jnp.where(bit == 1, got[n], buf)
                high = jnp.where(bit == 1, buf, got[n])
                bufs[key] = jnp.stack([low, high])
    out = []
    for r in range(rounds):
        segs = []
        for p in range(parts):
            perm = [nbits - 1 - (m.bit_length() - 1) for m in orders[p]]
            inverse = [perm.index(k) for k in range(nbits)] + [nbits, nbits + 1]
            segs.append(jnp.transpose(bufs[p, r], inverse).reshape(piece * size, chans))
        out.append(jnp.concatenate(segs, axis=0))
    return jnp.stack(out)


def correlate_kernel(meta_ref, blk_ref, ext_ref, corr_ref, power_ref):
    step = pl.program_id(0)
    chans = blk_ref.shape[2]
    width = ext_ref.shape[1]
    group = corr_ref.shape[1]
    lags = corr_ref.shape[2]
    tap = lax.broadcasted_iota(jnp.int32, (L, REACH), 0)
    col = lax.broadcasted_iota(jnp.int32, (L, REACH), 1)
    lane = lax.broadcasted_iota(jnp.int32, (L, chans), 1)
    pieces = []
    for g in range(group):
        idx = step * group + g
        first = meta_ref[4 * idx]
        shift = meta_ref[4 * idx + 1]
        lower = meta_ref[4 * idx + 2]
        upper = meta_ref[4 * idx + 3]
        rows = blk_ref[0, pl.ds(pl.multiple_of(first, 16), REACH), :]
        pick = (col == shift + (L - 1) - tap).astype(jnp.bfloat16)
        chosen = jnp.dot(pick, rows, preferred_element_type=jnp.float32)
        chosen = jnp.where((lane >= lower) & (lane < upper), chosen, 0.0)
        power_ref[0, g : g + 1, :] = jnp.full((1, 128), jnp.sum(chosen * chosen), jnp.float32)
        pieces.append(chosen.astype(jnp.bfloat16))
    product = jnp.dot(
        jnp.concatenate(pieces, axis=0), ext_ref[...], preferred_element_type=jnp.float32
    )
    for g in range(group):
        rows = product[g * L : (g + 1) * L]
        sheared = pltpu.roll(rows, width - (L - 1), 1, stride=1, stride_axis=0)
        corr_ref[0, g : g + 1, :] = jnp.sum(sheared, axis=0, keepdims=True)[:, :lags]


def correlate(meta, blocks, extended, count):
    rounds, span, chans = blocks.shape
    width = extended.shape[1]
    lag_count = span
    steps = rounds * count // GROUP
    per_round = count // GROUP
    cost = pl.CostEstimate(
        flops=2 * rounds * count * L * (chans * width + REACH * chans),
        transcendentals=0,
        bytes_accessed=blocks.size * 2 + extended.size * 2 + rounds * count * lag_count * 4,
    )
    grid_spec = pltpu.PrefetchScalarGridSpec(
        num_scalar_prefetch=1,
        grid=(steps,),
        in_specs=[
            pl.BlockSpec((1, span, chans), lambda i, m: (i // per_round, 0, 0)),
            pl.BlockSpec((chans, width), lambda i, m: (0, 0)),
        ],
        out_specs=[
            pl.BlockSpec((1, GROUP, lag_count), lambda i, m: (i, 0, 0)),
            pl.BlockSpec((1, GROUP, 128), lambda i, m: (i, 0, 0)),
        ],
    )
    corr, power = pl.pallas_call(
        correlate_kernel,
        grid_spec=grid_spec,
        out_shape=[
            jax.ShapeDtypeStruct((steps, GROUP, lag_count), jnp.float32),
            jax.ShapeDtypeStruct((steps, GROUP, 128), jnp.float32),
        ],
        cost_estimate=cost,
    )(meta, blocks, extended)
    return corr.reshape(rounds * count, lag_count), power[:, :, 0].reshape(rounds * count)


def window_sum(values, taps, lag_count):
    span = 1
    while span < taps:
        values = values[:, :-span] + values[:, span:]
        span *= 2
    return values[:, :lag_count]


def shards(signal, round_shard, offsets, chan_range):
    chan_local, lag_count = signal.shape
    rounds, count = offsets.shape
    section = lax.axis_index("sec")
    place = lax.axis_index("tm")
    total_lags = lag_count * lax.axis_size("tm")

    right_rim = from_behind(signal[:, :L], "tm", -1)
    extended = jnp.concatenate([signal, right_rim], axis=1)
    channel = section * chan_local + jnp.arange(chan_local, dtype=jnp.int32)
    lower = chan_range[:, :, 0]
    upper = chan_range[:, :, 1]
    inside = (channel >= lower[:, :, None]) & (channel < upper[:, :, None])

    blocks = spread_blocks(jnp.transpose(signal), round_shard, "tm")
    offs = jnp.clip(offsets, 0, lag_count - L)
    first = jnp.minimum((offs // 16) * 16, lag_count - REACH)
    base = section * chan_local
    meta = jnp.stack([first, offs - first, lower - base, upper - base], axis=-1).reshape(-1)

    squares = jnp.square(extended.astype(jnp.float32))
    high = lax.reduce_precision(squares, exponent_bits=8, mantissa_bits=7)
    low = (squares - high).astype(jnp.bfloat16)
    masks = inside.reshape(rounds * count, chan_local).astype(jnp.bfloat16)
    summed = jnp.dot(masks, high.astype(jnp.bfloat16), preferred_element_type=jnp.float32)
    summed = summed + jnp.dot(masks, low, preferred_element_type=jnp.float32)
    energy_local = window_sum(summed, L, lag_count)

    meta = meta.astype(jnp.int32).reshape(rounds, -1)
    energy = group_sum(energy_local, "sec").reshape(rounds, count, lag_count)
    normed, power = [], []
    for r in range(rounds):
        corr_local, local_power = correlate(meta[r], blocks[r : r + 1], extended, count)
        corr = group_sum(corr_local, "sec")
        tmpl_power = group_sum(local_power, "sec")
        cc = corr / jnp.sqrt(energy[r] * tmpl_power[:, None] + EPS)
        normed.append(cc)
        power.append(jnp.sum(cc * cc, axis=1))
    power_sum = group_sum(jnp.stack(power), "tm")
    meansq = power_sum / total_lags
    scored = jnp.stack(normed) / jnp.sqrt(meansq[:, :, None] + EPS)
    return scored.reshape(rounds, count, lag_count)


def solution(mesh):
    placed = (P("sec", "tm"), P(), P(), P())
    return jax.shard_map(
        shards, mesh=mesh, in_specs=placed, out_specs=P(None, None, "tm"), check_vma=False
    )
```

```python
import jax
import jax.numpy as jnp
from jax import lax
from jax.experimental import pallas as pl
from jax.experimental.pallas import tpu as pltpu
from jax.sharding import PartitionSpec as P

L = 128
GROUP = 4
REACH = L + 16

EPS = 1e-06


def from_behind(value, axis, by):
    length = lax.axis_size(axis)
    pairs = [(i, i + by) for i in range(length) if 0 <= i + by < length]
    return lax.ppermute(value, axis, pairs)


def group_sum(value, axis):
    size = lax.axis_size(axis)
    place = lax.axis_index(axis)
    stride = 1
    while stride < size:
        fan = 4 if size % (stride * 4) == 0 else 2 if size % (stride * 2) == 0 else 0
        if fan == 0:
            return lax.psum(value, axis)
        member = (place // stride) % fan
        got = {0: value}
        for d in range(1, fan):
            pairs = [(i, i ^ (d * stride)) for i in range(size)]
            got[d] = lax.ppermute(value, axis, pairs)
        total = None
        for m in range(fan):
            part = got[0]
            for d in range(1, fan):
                part = jnp.where((member ^ d) == m, got[d], part)
            total = part if total is None else total + part
        value = total
        stride *= fan
    return value


def spread_blocks(block, roots, axis):
    size = lax.axis_size(axis)
    place = lax.axis_index(axis)
    nbits = size.bit_length() - 1
    rounds = roots.shape[0]
    rows, chans = block.shape
    parts = next(p for p in (4, 2, 1) if rows % (p * size) == 0)
    if size & (size - 1) or rows % (parts * size) or nbits == 0:
        own = place == roots
        masked = jnp.where(own[:, None, None], block[None], jnp.zeros_like(block)[None])
        return lax.psum(masked, axis)
    piece = rows // (parts * size)
    low_bits = max(nbits - 1, 1)
    orders = [[1 << ((p + s) % low_bits) for s in range(low_bits)] for p in range(parts)]
    orders = [o + [1 << (nbits - 1)] if nbits > 1 else o for o in orders]
    bufs = {}
    for p in range(parts):
        seg = block[p * piece * size : (p + 1) * piece * size].reshape([2] * nbits + [piece, chans])
        perm = [nbits - 1 - (m.bit_length() - 1) for m in orders[p]] + [nbits, nbits + 1]
        seg = jnp.transpose(seg, perm)
        for r in range(rounds):
            bufs[p, r] = seg
    for s in range(nbits):
        sends, keeps = {}, {}
        for (p, r), buf in bufs.items():
            mask = orders[p][s]
            bit = (place // mask) % 2
            keeps[p, r] = jnp.where(bit == 1, buf[1], buf[0])
            sends.setdefault(mask, []).append(((p, r), jnp.where(bit == 1, buf[0], buf[1])))
        for mask, items in sends.items():
            got = lax.ppermute(jnp.stack([v for _, v in items]), axis, [(i, i ^ mask) for i in range(size)])
            for n, (key, _) in enumerate(items):
                held = sum(orders[key[0]][:s])
                holder = ((place ^ roots[key[1]]) & (size - 1 - held)) == 0
                bufs[key] = jnp.where(holder, keeps[key], got[n])
    for s in reversed(range(nbits)):
        sends = {}
        for (p, r), buf in bufs.items():
            sends.setdefault((r if s == 0 else 0, orders[p][s]), []).append(((p, r), buf))
        for (_, mask), items in sorted(sends.items()):
            got = lax.ppermute(jnp.stack([v for _, v in items]), axis, [(i, i ^ mask) for i in range(size)])
            bit = (place // mask) % 2
            for n, (key, buf) in enumerate(items):
                low = jnp.where(bit == 1, got[n], buf)
                high = jnp.where(bit == 1, buf, got[n])
                bufs[key] = jnp.stack([low, high])
    out = []
    for r in range(rounds):
        segs = []
        for p in range(parts):
            perm = [nbits - 1 - (m.bit_length() - 1) for m in orders[p]]
            inverse = [perm.index(k) for k in range(nbits)] + [nbits, nbits + 1]
            segs.append(jnp.transpose(bufs[p, r], inverse).reshape(piece * size, chans))
        out.append(jnp.concatenate(segs, axis=0))
    return jnp.stack(out)


def correlate_kernel(meta_ref, blk_ref, ext_ref, corr_ref, power_ref):
    step = pl.program_id(0)
    chans = blk_ref.shape[2]
    width = ext_ref.shape[1]
    group = corr_ref.shape[1]
    lags = corr_ref.shape[2]
    tap = lax.broadcasted_iota(jnp.int32, (L, REACH), 0)
    col = lax.broadcasted_iota(jnp.int32, (L, REACH), 1)
    lane = lax.broadcasted_iota(jnp.int32, (L, chans), 1)
    pieces = []
    for g in range(group):
        idx = step * group + g
        first = meta_ref[4 * idx]
        shift = meta_ref[4 * idx + 1]
        lower = meta_ref[4 * idx + 2]
        upper = meta_ref[4 * idx + 3]
        rows = blk_ref[0, pl.ds(pl.multiple_of(first, 16), REACH), :]
        pick = (col == shift + (L - 1) - tap).astype(jnp.bfloat16)
        chosen = jnp.dot(pick, rows, preferred_element_type=jnp.float32)
        chosen = jnp.where((lane >= lower) & (lane < upper), chosen, 0.0)
        power_ref[0, g : g + 1, :] = jnp.full((1, 128), jnp.sum(chosen * chosen), jnp.float32)
        pieces.append(chosen.astype(jnp.bfloat16))
    product = jnp.dot(
        jnp.concatenate(pieces, axis=0), ext_ref[...], preferred_element_type=jnp.float32
    )
    for g in range(group):
        rows = product[g * L : (g + 1) * L]
        sheared = pltpu.roll(rows, width - (L - 1), 1, stride=1, stride_axis=0)
        corr_ref[0, g : g + 1, :] = jnp.sum(sheared, axis=0, keepdims=True)[:, :lags]


def correlate(meta, blocks, extended, count):
    rounds, span, chans = blocks.shape
    width = extended.shape[1]
    lag_count = span
    steps = rounds * count // GROUP
    per_round = count // GROUP
    cost = pl.CostEstimate(
        flops=2 * rounds * count * L * (chans * width + REACH * chans),
        transcendentals=0,
        bytes_accessed=blocks.size * 2 + extended.size * 2 + rounds * count * lag_count * 4,
    )
    grid_spec = pltpu.PrefetchScalarGridSpec(
        num_scalar_prefetch=1,
        grid=(steps,),
        in_specs=[
            pl.BlockSpec((1, span, chans), lambda i, m: (i // per_round, 0, 0)),
            pl.BlockSpec((chans, width), lambda i, m: (0, 0)),
        ],
        out_specs=[
            pl.BlockSpec((1, GROUP, lag_count), lambda i, m: (i, 0, 0)),
            pl.BlockSpec((1, GROUP, 128), lambda i, m: (i, 0, 0)),
        ],
    )
    corr, power = pl.pallas_call(
        correlate_kernel,
        grid_spec=grid_spec,
        out_shape=[
            jax.ShapeDtypeStruct((steps, GROUP, lag_count), jnp.float32),
            jax.ShapeDtypeStruct((steps, GROUP, 128), jnp.float32),
        ],
        cost_estimate=cost,
    )(meta, blocks, extended)
    return corr.reshape(rounds * count, lag_count), power[:, :, 0].reshape(rounds * count)


def window_sum(values, taps, lag_count):
    span = 1
    while span < taps:
        values = values[:, :-span] + values[:, span:]
        span *= 2
    return values[:, :lag_count]


def shards(signal, round_shard, offsets, chan_range):
    chan_local, lag_count = signal.shape
    rounds, count = offsets.shape
    section = lax.axis_index("sec")
    place = lax.axis_index("tm")
    total_lags = lag_count * lax.axis_size("tm")

    right_rim = from_behind(signal[:, :L], "tm", -1)
    extended = jnp.concatenate([signal, right_rim], axis=1)
    channel = section * chan_local + jnp.arange(chan_local, dtype=jnp.int32)
    lower = chan_range[:, :, 0]
    upper = chan_range[:, :, 1]
    inside = (channel >= lower[:, :, None]) & (channel < upper[:, :, None])

    blocks = spread_blocks(jnp.transpose(signal), round_shard, "tm")
    offs = jnp.clip(offsets, 0, lag_count - L)
    first = jnp.minimum((offs // 16) * 16, lag_count - REACH)
    base = section * chan_local
    meta = jnp.stack([first, offs - first, lower - base, upper - base], axis=-1).reshape(-1)

    squares = jnp.square(extended.astype(jnp.float32))
    high = lax.reduce_precision(squares, exponent_bits=8, mantissa_bits=7)
    low = (squares - high).astype(jnp.bfloat16)
    masks = inside.reshape(rounds * count, chan_local).astype(jnp.bfloat16)
    summed = jnp.dot(masks, high.astype(jnp.bfloat16), preferred_element_type=jnp.float32)
    summed = summed + jnp.dot(masks, low, preferred_element_type=jnp.float32)
    energy_local = window_sum(summed, L, lag_count)

    meta = meta.astype(jnp.int32).reshape(rounds, -1)
    pieces = [correlate(meta[r], blocks[r : r + 1], extended, count) for r in range(rounds)]
    corr_local = jnp.concatenate([c for c, _ in pieces])
    local_power = jnp.concatenate([p for _, p in pieces])
    tmpl_power = group_sum(local_power, "sec")
    both = group_sum(jnp.stack([corr_local, energy_local]), "sec")
    corr, energy = both[0], both[1]
    normed = corr / jnp.sqrt(energy * tmpl_power[:, None] + EPS)
    power_sum = group_sum(jnp.sum(normed * normed, axis=1), "tm")
    meansq = power_sum / total_lags
    scored = normed / jnp.sqrt(meansq[:, None] + EPS)
    return scored.reshape(rounds, count, lag_count)


def solution(mesh):
    placed = (P("sec", "tm"), P(), P(), P())
    return jax.shard_map(
        shards, mesh=mesh, in_specs=placed, out_specs=P(None, None, "tm"), check_vma=False
    )
```

```python
import jax
import jax.numpy as jnp
from jax import lax
from jax.experimental import pallas as pl
from jax.experimental.pallas import tpu as pltpu
from jax.sharding import PartitionSpec as P

L = 128
GROUP = 4
REACH = L + 16

EPS = 1e-06


def from_behind(value, axis, by):
    length = lax.axis_size(axis)
    pairs = [(i, i + by) for i in range(length) if 0 <= i + by < length]
    return lax.ppermute(value, axis, pairs)


def group_sum(value, axis):
    size = lax.axis_size(axis)
    place = lax.axis_index(axis)
    stride = 1
    while stride < size:
        fan = 4 if size % (stride * 4) == 0 else 2 if size % (stride * 2) == 0 else 0
        if fan == 0:
            return lax.psum(value, axis)
        member = (place // stride) % fan
        got = {0: value}
        for d in range(1, fan):
            pairs = [(i, i ^ (d * stride)) for i in range(size)]
            got[d] = lax.ppermute(value, axis, pairs)
        total = None
        for m in range(fan):
            part = got[0]
            for d in range(1, fan):
                part = jnp.where((member ^ d) == m, got[d], part)
            total = part if total is None else total + part
        value = total
        stride *= fan
    return value


def spread_blocks(block, roots, axis):
    size = lax.axis_size(axis)
    place = lax.axis_index(axis)
    nbits = size.bit_length() - 1
    rounds = roots.shape[0]
    rows, chans = block.shape
    parts = next(p for p in (4, 2, 1) if rows % (p * size) == 0)
    if size & (size - 1) or rows % (parts * size) or nbits == 0:
        own = place == roots
        masked = jnp.where(own[:, None, None], block[None], jnp.zeros_like(block)[None])
        return lax.psum(masked, axis)
    piece = rows // (parts * size)
    orders = [[1 << ((p + s) % nbits) for s in range(nbits)] for p in range(parts)]
    bufs = {}
    for p in range(parts):
        seg = block[p * piece * size : (p + 1) * piece * size].reshape([2] * nbits + [piece, chans])
        perm = [nbits - 1 - (m.bit_length() - 1) for m in orders[p]] + [nbits, nbits + 1]
        seg = jnp.transpose(seg, perm)
        for r in range(rounds):
            bufs[p, r] = seg
    for s in range(nbits):
        sends, keeps = {}, {}
        for (p, r), buf in bufs.items():
            mask = orders[p][s]
            bit = (place // mask) % 2
            keeps[p, r] = jnp.where(bit == 1, buf[1], buf[0])
            sends.setdefault(mask, []).append(((p, r), jnp.where(bit == 1, buf[0], buf[1])))
        for mask, items in sorted(sends.items(), key=lambda kv: -kv[0]):
            got = lax.ppermute(jnp.stack([v for _, v in items]), axis, [(i, i ^ mask) for i in range(size)])
            for n, (key, _) in enumerate(items):
                held = sum(orders[key[0]][:s])
                holder = ((place ^ roots[key[1]]) & (size - 1 - held)) == 0
                bufs[key] = jnp.where(holder, keeps[key], got[n])
    for s in reversed(range(nbits)):
        sends = {}
        for (p, r), buf in bufs.items():
            sends.setdefault((r if s == 0 else 0, orders[p][s]), []).append(((p, r), buf))
        for (_, mask), items in sorted(sends.items(), key=lambda kv: (kv[0][0], -kv[0][1])):
            got = lax.ppermute(jnp.stack([v for _, v in items]), axis, [(i, i ^ mask) for i in range(size)])
            bit = (place // mask) % 2
            for n, (key, buf) in enumerate(items):
                low = jnp.where(bit == 1, got[n], buf)
                high = jnp.where(bit == 1, buf, got[n])
                bufs[key] = jnp.stack([low, high])
    out = []
    for r in range(rounds):
        segs = []
        for p in range(parts):
            perm = [nbits - 1 - (m.bit_length() - 1) for m in orders[p]]
            inverse = [perm.index(k) for k in range(nbits)] + [nbits, nbits + 1]
            segs.append(jnp.transpose(bufs[p, r], inverse).reshape(piece * size, chans))
        out.append(jnp.concatenate(segs, axis=0))
    return jnp.stack(out)


def correlate_kernel(meta_ref, blk_ref, ext_ref, corr_ref, power_ref):
    step = pl.program_id(0)
    chans = blk_ref.shape[2]
    width = ext_ref.shape[1]
    group = corr_ref.shape[1]
    lags = corr_ref.shape[2]
    tap = lax.broadcasted_iota(jnp.int32, (L, REACH), 0)
    col = lax.broadcasted_iota(jnp.int32, (L, REACH), 1)
    lane = lax.broadcasted_iota(jnp.int32, (L, chans), 1)
    pieces = []
    for g in range(group):
        idx = step * group + g
        first = meta_ref[4 * idx]
        shift = meta_ref[4 * idx + 1]
        lower = meta_ref[4 * idx + 2]
        upper = meta_ref[4 * idx + 3]
        rows = blk_ref[0, pl.ds(pl.multiple_of(first, 16), REACH), :]
        pick = (col == shift + (L - 1) - tap).astype(jnp.bfloat16)
        chosen = jnp.dot(pick, rows, preferred_element_type=jnp.float32)
        chosen = jnp.where((lane >= lower) & (lane < upper), chosen, 0.0)
        power_ref[0, g : g + 1, :] = jnp.full((1, 128), jnp.sum(chosen * chosen), jnp.float32)
        pieces.append(chosen.astype(jnp.bfloat16))
    product = jnp.dot(
        jnp.concatenate(pieces, axis=0), ext_ref[...], preferred_element_type=jnp.float32
    )
    for g in range(group):
        rows = product[g * L : (g + 1) * L]
        sheared = pltpu.roll(rows, width - (L - 1), 1, stride=1, stride_axis=0)
        corr_ref[0, g : g + 1, :] = jnp.sum(sheared, axis=0, keepdims=True)[:, :lags]


def correlate(meta, blocks, extended, count):
    rounds, span, chans = blocks.shape
    width = extended.shape[1]
    lag_count = span
    steps = rounds * count // GROUP
    per_round = count // GROUP
    cost = pl.CostEstimate(
        flops=2 * rounds * count * L * (chans * width + REACH * chans),
        transcendentals=0,
        bytes_accessed=blocks.size * 2 + extended.size * 2 + rounds * count * lag_count * 4,
    )
    grid_spec = pltpu.PrefetchScalarGridSpec(
        num_scalar_prefetch=1,
        grid=(steps,),
        in_specs=[
            pl.BlockSpec((1, span, chans), lambda i, m: (i // per_round, 0, 0)),
            pl.BlockSpec((chans, width), lambda i, m: (0, 0)),
        ],
        out_specs=[
            pl.BlockSpec((1, GROUP, lag_count), lambda i, m: (i, 0, 0)),
            pl.BlockSpec((1, GROUP, 128), lambda i, m: (i, 0, 0)),
        ],
    )
    corr, power = pl.pallas_call(
        correlate_kernel,
        grid_spec=grid_spec,
        out_shape=[
            jax.ShapeDtypeStruct((steps, GROUP, lag_count), jnp.float32),
            jax.ShapeDtypeStruct((steps, GROUP, 128), jnp.float32),
        ],
        cost_estimate=cost,
    )(meta, blocks, extended)
    return corr.reshape(rounds * count, lag_count), power[:, :, 0].reshape(rounds * count)


def window_sum(values, taps, lag_count):
    span = 1
    while span < taps:
        values = values[:, :-span] + values[:, span:]
        span *= 2
    return values[:, :lag_count]


def shards(signal, round_shard, offsets, chan_range):
    chan_local, lag_count = signal.shape
    rounds, count = offsets.shape
    section = lax.axis_index("sec")
    place = lax.axis_index("tm")
    total_lags = lag_count * lax.axis_size("tm")

    right_rim = from_behind(signal[:, :L], "tm", -1)
    extended = jnp.concatenate([signal, right_rim], axis=1)
    channel = section * chan_local + jnp.arange(chan_local, dtype=jnp.int32)
    lower = chan_range[:, :, 0]
    upper = chan_range[:, :, 1]
    inside = (channel >= lower[:, :, None]) & (channel < upper[:, :, None])

    blocks = spread_blocks(jnp.transpose(signal), round_shard, "tm")
    offs = jnp.clip(offsets, 0, lag_count - L)
    first = jnp.minimum((offs // 16) * 16, lag_count - REACH)
    base = section * chan_local
    meta = jnp.stack([first, offs - first, lower - base, upper - base], axis=-1).reshape(-1)

    squares = jnp.square(extended.astype(jnp.float32))
    high = lax.reduce_precision(squares, exponent_bits=8, mantissa_bits=7)
    low = (squares - high).astype(jnp.bfloat16)
    masks = inside.reshape(rounds * count, chan_local).astype(jnp.bfloat16)
    summed = jnp.dot(masks, high.astype(jnp.bfloat16), preferred_element_type=jnp.float32)
    summed = summed + jnp.dot(masks, low, preferred_element_type=jnp.float32)
    energy_local = window_sum(summed, L, lag_count)

    meta = meta.astype(jnp.int32).reshape(rounds, -1)
    pieces = [correlate(meta[r], blocks[r : r + 1], extended, count) for r in range(rounds)]
    corr_local = jnp.concatenate([c for c, _ in pieces])
    local_power = jnp.concatenate([p for _, p in pieces])
    tmpl_power = group_sum(local_power, "sec")
    both = group_sum(jnp.stack([corr_local, energy_local]), "sec")
    corr, energy = both[0], both[1]
    normed = corr / jnp.sqrt(energy * tmpl_power[:, None] + EPS)
    power_sum = group_sum(jnp.sum(normed * normed, axis=1), "tm")
    meansq = power_sum / total_lags
    scored = normed / jnp.sqrt(meansq[:, None] + EPS)
    return scored.reshape(rounds, count, lag_count)


def solution(mesh):
    placed = (P("sec", "tm"), P(), P(), P())
    return jax.shard_map(
        shards, mesh=mesh, in_specs=placed, out_specs=P(None, None, "tm"), check_vma=False
    )
```

```python
import jax
import jax.numpy as jnp
from jax import lax
from jax.experimental import pallas as pl
from jax.experimental.pallas import tpu as pltpu
from jax.sharding import PartitionSpec as P

L = 128
GROUP = 4
REACH = L + 16

EPS = 1e-06


def from_behind(value, axis, by):
    length = lax.axis_size(axis)
    pairs = [(i, i + by) for i in range(length) if 0 <= i + by < length]
    return lax.ppermute(value, axis, pairs)


def group_sum(value, axis):
    size = lax.axis_size(axis)
    place = lax.axis_index(axis)
    stride = 1
    while stride < size:
        fan = 4 if size % (stride * 4) == 0 else 2 if size % (stride * 2) == 0 else 0
        if fan == 0:
            return lax.psum(value, axis)
        member = (place // stride) % fan
        got = {0: value}
        for d in range(1, fan):
            pairs = [(i, i ^ (d * stride)) for i in range(size)]
            got[d] = lax.ppermute(value, axis, pairs)
        total = None
        for m in range(fan):
            part = got[0]
            for d in range(1, fan):
                part = jnp.where((member ^ d) == m, got[d], part)
            total = part if total is None else total + part
        value = total
        stride *= fan
    return value


def spread_blocks(block, roots, axis):
    size = lax.axis_size(axis)
    place = lax.axis_index(axis)
    nbits = size.bit_length() - 1
    rounds = roots.shape[0]
    rows, chans = block.shape
    parts = next(p for p in (4, 2, 1) if rows % (p * size) == 0)
    if size & (size - 1) or rows % (parts * size) or nbits == 0:
        own = place == roots
        masked = jnp.where(own[:, None, None], block[None], jnp.zeros_like(block)[None])
        return lax.psum(masked, axis)
    piece = rows // (parts * size)
    orders = [[1 << ((p + s) % nbits) for s in range(nbits)] for p in range(parts)]
    bufs = {}
    for p in range(parts):
        seg = block[p * piece * size : (p + 1) * piece * size].reshape([2] * nbits + [piece, chans])
        perm = [nbits - 1 - (m.bit_length() - 1) for m in orders[p]] + [nbits, nbits + 1]
        seg = jnp.transpose(seg, perm)
        for r in range(rounds):
            bufs[p, r] = seg
    for s in range(nbits):
        sends, keeps = {}, {}
        for (p, r), buf in bufs.items():
            mask = orders[p][s]
            bit = (place // mask) % 2
            keeps[p, r] = jnp.where(bit == 1, buf[1], buf[0])
            sends.setdefault(mask, []).append(((p, r), jnp.where(bit == 1, buf[0], buf[1])))
        for mask, items in sorted(sends.items(), key=lambda kv: -kv[0]):
            got = lax.ppermute(jnp.stack([v for _, v in items]), axis, [(i, i ^ mask) for i in range(size)])
            for n, (key, _) in enumerate(items):
                held = sum(orders[key[0]][:s])
                holder = ((place ^ roots[key[1]]) & (size - 1 - held)) == 0
                bufs[key] = jnp.where(holder, keeps[key], got[n])
    for s in reversed(range(nbits)):
        sends = {}
        for (p, r), buf in bufs.items():
            sends.setdefault((r if s <= 1 else 0, orders[p][s]), []).append(((p, r), buf))
        for (_, mask), items in sorted(sends.items(), key=lambda kv: (kv[0][0], -kv[0][1])):
            got = lax.ppermute(jnp.stack([v for _, v in items]), axis, [(i, i ^ mask) for i in range(size)])
            bit = (place // mask) % 2
            for n, (key, buf) in enumerate(items):
                low = jnp.where(bit == 1, got[n], buf)
                high = jnp.where(bit == 1, buf, got[n])
                bufs[key] = jnp.stack([low, high])
    out = []
    for r in range(rounds):
        segs = []
        for p in range(parts):
            perm = [nbits - 1 - (m.bit_length() - 1) for m in orders[p]]
            inverse = [perm.index(k) for k in range(nbits)] + [nbits, nbits + 1]
            segs.append(jnp.transpose(bufs[p, r], inverse).reshape(piece * size, chans))
        out.append(jnp.concatenate(segs, axis=0))
    return jnp.stack(out)


def correlate_kernel(meta_ref, blk_ref, ext_ref, corr_ref, power_ref):
    step = pl.program_id(0)
    chans = blk_ref.shape[2]
    width = ext_ref.shape[1]
    group = corr_ref.shape[1]
    lags = corr_ref.shape[2]
    tap = lax.broadcasted_iota(jnp.int32, (L, REACH), 0)
    col = lax.broadcasted_iota(jnp.int32, (L, REACH), 1)
    lane = lax.broadcasted_iota(jnp.int32, (L, chans), 1)
    pieces = []
    for g in range(group):
        idx = step * group + g
        first = meta_ref[4 * idx]
        shift = meta_ref[4 * idx + 1]
        lower = meta_ref[4 * idx + 2]
        upper = meta_ref[4 * idx + 3]
        rows = blk_ref[0, pl.ds(pl.multiple_of(first, 16), REACH), :]
        pick = (col == shift + (L - 1) - tap).astype(jnp.bfloat16)
        chosen = jnp.dot(pick, rows, preferred_element_type=jnp.float32)
        chosen = jnp.where((lane >= lower) & (lane < upper), chosen, 0.0)
        power_ref[0, g : g + 1, :] = jnp.full((1, 128), jnp.sum(chosen * chosen), jnp.float32)
        pieces.append(chosen.astype(jnp.bfloat16))
    product = jnp.dot(
        jnp.concatenate(pieces, axis=0), ext_ref[...], preferred_element_type=jnp.float32
    )
    for g in range(group):
        rows = product[g * L : (g + 1) * L]
        sheared = pltpu.roll(rows, width - (L - 1), 1, stride=1, stride_axis=0)
        corr_ref[0, g : g + 1, :] = jnp.sum(sheared, axis=0, keepdims=True)[:, :lags]


def correlate(meta, blocks, extended, count):
    rounds, span, chans = blocks.shape
    width = extended.shape[1]
    lag_count = span
    steps = rounds * count // GROUP
    per_round = count // GROUP
    cost = pl.CostEstimate(
        flops=2 * rounds * count * L * (chans * width + REACH * chans),
        transcendentals=0,
        bytes_accessed=blocks.size * 2 + extended.size * 2 + rounds * count * lag_count * 4,
    )
    grid_spec = pltpu.PrefetchScalarGridSpec(
        num_scalar_prefetch=1,
        grid=(steps,),
        in_specs=[
            pl.BlockSpec((1, span, chans), lambda i, m: (i // per_round, 0, 0)),
            pl.BlockSpec((chans, width), lambda i, m: (0, 0)),
        ],
        out_specs=[
            pl.BlockSpec((1, GROUP, lag_count), lambda i, m: (i, 0, 0)),
            pl.BlockSpec((1, GROUP, 128), lambda i, m: (i, 0, 0)),
        ],
    )
    corr, power = pl.pallas_call(
        correlate_kernel,
        grid_spec=grid_spec,
        out_shape=[
            jax.ShapeDtypeStruct((steps, GROUP, lag_count), jnp.float32),
            jax.ShapeDtypeStruct((steps, GROUP, 128), jnp.float32),
        ],
        cost_estimate=cost,
    )(meta, blocks, extended)
    return corr.reshape(rounds * count, lag_count), power[:, :, 0].reshape(rounds * count)


def window_sum(values, taps, lag_count):
    span = 1
    while span < taps:
        values = values[:, :-span] + values[:, span:]
        span *= 2
    return values[:, :lag_count]


def shards(signal, round_shard, offsets, chan_range):
    chan_local, lag_count = signal.shape
    rounds, count = offsets.shape
    section = lax.axis_index("sec")
    place = lax.axis_index("tm")
    total_lags = lag_count * lax.axis_size("tm")

    right_rim = from_behind(signal[:, :L], "tm", -1)
    extended = jnp.concatenate([signal, right_rim], axis=1)
    channel = section * chan_local + jnp.arange(chan_local, dtype=jnp.int32)
    lower = chan_range[:, :, 0]
    upper = chan_range[:, :, 1]
    inside = (channel >= lower[:, :, None]) & (channel < upper[:, :, None])

    blocks = spread_blocks(jnp.transpose(signal), round_shard, "tm")
    offs = jnp.clip(offsets, 0, lag_count - L)
    first = jnp.minimum((offs // 16) * 16, lag_count - REACH)
    base = section * chan_local
    meta = jnp.stack([first, offs - first, lower - base, upper - base], axis=-1).reshape(-1)

    squares = jnp.square(extended.astype(jnp.float32))
    high = lax.reduce_precision(squares, exponent_bits=8, mantissa_bits=7)
    low = (squares - high).astype(jnp.bfloat16)
    masks = inside.reshape(rounds * count, chan_local).astype(jnp.bfloat16)
    summed = jnp.dot(masks, high.astype(jnp.bfloat16), preferred_element_type=jnp.float32)
    summed = summed + jnp.dot(masks, low, preferred_element_type=jnp.float32)
    energy_local = window_sum(summed, L, lag_count)

    meta = meta.astype(jnp.int32).reshape(rounds, -1)
    pieces = [correlate(meta[r], blocks[r : r + 1], extended, count) for r in range(rounds)]
    corr_local = jnp.concatenate([c for c, _ in pieces])
    local_power = jnp.concatenate([p for _, p in pieces])
    tmpl_power = group_sum(local_power, "sec")
    both = group_sum(jnp.stack([corr_local, energy_local]), "sec")
    corr, energy = both[0], both[1]
    normed = corr / jnp.sqrt(energy * tmpl_power[:, None] + EPS)
    power_sum = group_sum(jnp.sum(normed * normed, axis=1), "tm")
    meansq = power_sum / total_lags
    scored = normed / jnp.sqrt(meansq[:, None] + EPS)
    return scored.reshape(rounds, count, lag_count)


def solution(mesh):
    placed = (P("sec", "tm"), P(), P(), P())
    return jax.shard_map(
        shards, mesh=mesh, in_specs=placed, out_specs=P(None, None, "tm"), check_vma=False
    )
```

```python
import jax
import jax.numpy as jnp
from jax import lax
from jax.experimental import pallas as pl
from jax.experimental.pallas import tpu as pltpu
from jax.sharding import PartitionSpec as P

L = 128
GROUP = 4
REACH = L + 16

EPS = 1e-06


def from_behind(value, axis, by):
    length = lax.axis_size(axis)
    pairs = [(i, i + by) for i in range(length) if 0 <= i + by < length]
    return lax.ppermute(value, axis, pairs)


def group_sum(value, axis):
    size = lax.axis_size(axis)
    place = lax.axis_index(axis)
    stride = 1
    while stride < size:
        fan = 4 if stride == 1 and size % 4 == 0 else 2 if size % (stride * 2) == 0 else 0
        if fan == 0:
            return lax.psum(value, axis)
        member = (place // stride) % fan
        got = {0: value}
        for d in range(1, fan):
            pairs = [(i, i ^ (d * stride)) for i in range(size)]
            got[d] = lax.ppermute(value, axis, pairs)
        total = None
        for m in range(fan):
            part = got[0]
            for d in range(1, fan):
                part = jnp.where((member ^ d) == m, got[d], part)
            total = part if total is None else total + part
        value = total
        stride *= fan
    return value


def spread_blocks(block, roots, axis):
    size = lax.axis_size(axis)
    place = lax.axis_index(axis)
    nbits = size.bit_length() - 1
    rounds = roots.shape[0]
    rows, chans = block.shape
    parts = next(p for p in (4, 2, 1) if rows % (p * size) == 0)
    if size & (size - 1) or rows % (parts * size) or nbits == 0:
        own = place == roots
        masked = jnp.where(own[:, None, None], block[None], jnp.zeros_like(block)[None])
        return lax.psum(masked, axis)
    piece = rows // (parts * size)
    orders = [[1 << ((p + s) % nbits) for s in range(nbits)] for p in range(parts)]
    bufs = {}
    for p in range(parts):
        seg = block[p * piece * size : (p + 1) * piece * size].reshape([2] * nbits + [piece, chans])
        perm = [nbits - 1 - (m.bit_length() - 1) for m in orders[p]] + [nbits, nbits + 1]
        seg = jnp.transpose(seg, perm)
        for r in range(rounds):
            bufs[p, r] = seg
    for s in range(nbits):
        sends, keeps = {}, {}
        for (p, r), buf in bufs.items():
            mask = orders[p][s]
            bit = (place // mask) % 2
            keeps[p, r] = jnp.where(bit == 1, buf[1], buf[0])
            sends.setdefault(mask, []).append(((p, r), jnp.where(bit == 1, buf[0], buf[1])))
        for mask, items in sorted(sends.items(), key=lambda kv: -kv[0]):
            got = lax.ppermute(jnp.stack([v for _, v in items]), axis, [(i, i ^ mask) for i in range(size)])
            for n, (key, _) in enumerate(items):
                held = sum(orders[key[0]][:s])
                holder = ((place ^ roots[key[1]]) & (size - 1 - held)) == 0
                bufs[key] = jnp.where(holder, keeps[key], got[n])
    for s in reversed(range(nbits)):
        sends = {}
        for (p, r), buf in bufs.items():
            sends.setdefault((r if s == 0 else 0, orders[p][s]), []).append(((p, r), buf))
        for (_, mask), items in sorted(sends.items(), key=lambda kv: (kv[0][0], -kv[0][1])):
            got = lax.ppermute(jnp.stack([v for _, v in items]), axis, [(i, i ^ mask) for i in range(size)])
            bit = (place // mask) % 2
            for n, (key, buf) in enumerate(items):
                low = jnp.where(bit == 1, got[n], buf)
                high = jnp.where(bit == 1, buf, got[n])
                bufs[key] = jnp.stack([low, high])
    out = []
    for r in range(rounds):
        segs = []
        for p in range(parts):
            perm = [nbits - 1 - (m.bit_length() - 1) for m in orders[p]]
            inverse = [perm.index(k) for k in range(nbits)] + [nbits, nbits + 1]
            segs.append(jnp.transpose(bufs[p, r], inverse).reshape(piece * size, chans))
        out.append(jnp.concatenate(segs, axis=0))
    return jnp.stack(out)


def correlate_kernel(meta_ref, blk_ref, ext_ref, corr_ref, power_ref):
    step = pl.program_id(0)
    chans = blk_ref.shape[2]
    width = ext_ref.shape[1]
    group = corr_ref.shape[1]
    lags = corr_ref.shape[2]
    tap = lax.broadcasted_iota(jnp.int32, (L, REACH), 0)
    col = lax.broadcasted_iota(jnp.int32, (L, REACH), 1)
    lane = lax.broadcasted_iota(jnp.int32, (L, chans), 1)
    pieces = []
    for g in range(group):
        idx = step * group + g
        first = meta_ref[4 * idx]
        shift = meta_ref[4 * idx + 1]
        lower = meta_ref[4 * idx + 2]
        upper = meta_ref[4 * idx + 3]
        rows = blk_ref[0, pl.ds(pl.multiple_of(first, 16), REACH), :]
        pick = (col == shift + (L - 1) - tap).astype(jnp.bfloat16)
        chosen = jnp.dot(pick, rows, preferred_element_type=jnp.float32)
        chosen = jnp.where((lane >= lower) & (lane < upper), chosen, 0.0)
        power_ref[0, g : g + 1, :] = jnp.full((1, 128), jnp.sum(chosen * chosen), jnp.float32)
        pieces.append(chosen.astype(jnp.bfloat16))
    product = jnp.dot(
        jnp.concatenate(pieces, axis=0), ext_ref[...], preferred_element_type=jnp.float32
    )
    for g in range(group):
        rows = product[g * L : (g + 1) * L]
        sheared = pltpu.roll(rows, width - (L - 1), 1, stride=1, stride_axis=0)
        corr_ref[0, g : g + 1, :] = jnp.sum(sheared, axis=0, keepdims=True)[:, :lags]


def correlate(meta, blocks, extended, count):
    rounds, span, chans = blocks.shape
    width = extended.shape[1]
    lag_count = span
    steps = rounds * count // GROUP
    per_round = count // GROUP
    cost = pl.CostEstimate(
        flops=2 * rounds * count * L * (chans * width + REACH * chans),
        transcendentals=0,
        bytes_accessed=blocks.size * 2 + extended.size * 2 + rounds * count * lag_count * 4,
    )
    grid_spec = pltpu.PrefetchScalarGridSpec(
        num_scalar_prefetch=1,
        grid=(steps,),
        in_specs=[
            pl.BlockSpec((1, span, chans), lambda i, m: (i // per_round, 0, 0)),
            pl.BlockSpec((chans, width), lambda i, m: (0, 0)),
        ],
        out_specs=[
            pl.BlockSpec((1, GROUP, lag_count), lambda i, m: (i, 0, 0)),
            pl.BlockSpec((1, GROUP, 128), lambda i, m: (i, 0, 0)),
        ],
    )
    corr, power = pl.pallas_call(
        correlate_kernel,
        grid_spec=grid_spec,
        out_shape=[
            jax.ShapeDtypeStruct((steps, GROUP, lag_count), jnp.float32),
            jax.ShapeDtypeStruct((steps, GROUP, 128), jnp.float32),
        ],
        cost_estimate=cost,
    )(meta, blocks, extended)
    return corr.reshape(rounds * count, lag_count), power[:, :, 0].reshape(rounds * count)


def window_sum(values, taps, lag_count):
    span = 1
    while span < taps:
        values = values[:, :-span] + values[:, span:]
        span *= 2
    return values[:, :lag_count]


def shards(signal, round_shard, offsets, chan_range):
    chan_local, lag_count = signal.shape
    rounds, count = offsets.shape
    section = lax.axis_index("sec")
    place = lax.axis_index("tm")
    total_lags = lag_count * lax.axis_size("tm")

    right_rim = from_behind(signal[:, :L], "tm", -1)
    extended = jnp.concatenate([signal, right_rim], axis=1)
    channel = section * chan_local + jnp.arange(chan_local, dtype=jnp.int32)
    lower = chan_range[:, :, 0]
    upper = chan_range[:, :, 1]
    inside = (channel >= lower[:, :, None]) & (channel < upper[:, :, None])

    blocks = spread_blocks(jnp.transpose(signal), round_shard, "tm")
    offs = jnp.clip(offsets, 0, lag_count - L)
    first = jnp.minimum((offs // 16) * 16, lag_count - REACH)
    base = section * chan_local
    meta = jnp.stack([first, offs - first, lower - base, upper - base], axis=-1).reshape(-1)

    squares = jnp.square(extended.astype(jnp.float32))
    high = lax.reduce_precision(squares, exponent_bits=8, mantissa_bits=7)
    low = (squares - high).astype(jnp.bfloat16)
    masks = inside.reshape(rounds * count, chan_local).astype(jnp.bfloat16)
    summed = jnp.dot(masks, high.astype(jnp.bfloat16), preferred_element_type=jnp.float32)
    summed = summed + jnp.dot(masks, low, preferred_element_type=jnp.float32)
    energy_local = window_sum(summed, L, lag_count)

    meta = meta.astype(jnp.int32).reshape(rounds, -1)
    pieces = [correlate(meta[r], blocks[r : r + 1], extended, count) for r in range(rounds)]
    corr_local = jnp.concatenate([c for c, _ in pieces])
    local_power = jnp.concatenate([p for _, p in pieces])
    tmpl_power = group_sum(local_power, "sec")
    both = group_sum(jnp.stack([corr_local, energy_local]), "sec")
    corr, energy = both[0], both[1]
    normed = corr / jnp.sqrt(energy * tmpl_power[:, None] + EPS)
    power_sum = group_sum(jnp.sum(normed * normed, axis=1), "tm")
    meansq = power_sum / total_lags
    scored = normed / jnp.sqrt(meansq[:, None] + EPS)
    return scored.reshape(rounds, count, lag_count)


def solution(mesh):
    placed = (P("sec", "tm"), P(), P(), P())
    return jax.shard_map(
        shards, mesh=mesh, in_specs=placed, out_specs=P(None, None, "tm"), check_vma=False
    )
```

```python
import jax
import jax.numpy as jnp
from jax import lax
from jax.experimental import pallas as pl
from jax.experimental.pallas import tpu as pltpu
from jax.sharding import PartitionSpec as P

L = 128
GROUP = 4
REACH = L + 16

EPS = 1e-06


def from_behind(value, axis, by):
    length = lax.axis_size(axis)
    pairs = [(i, i + by) for i in range(length) if 0 <= i + by < length]
    return lax.ppermute(value, axis, pairs)


def group_sum(value, axis):
    size = lax.axis_size(axis)
    place = lax.axis_index(axis)
    stride = 1
    while stride < size:
        fan = 4 if size % (stride * 4) == 0 else 2 if size % (stride * 2) == 0 else 0
        if fan == 0:
            return lax.psum(value, axis)
        member = (place // stride) % fan
        got = {0: value}
        for d in range(1, fan):
            pairs = [(i, i ^ (d * stride)) for i in range(size)]
            got[d] = lax.ppermute(value, axis, pairs)
        total = None
        for m in range(fan):
            part = got[0]
            for d in range(1, fan):
                part = jnp.where((member ^ d) == m, got[d], part)
            total = part if total is None else total + part
        value = total
        stride *= fan
    return value


def spread_blocks(block, roots, axis):
    size = lax.axis_size(axis)
    place = lax.axis_index(axis)
    nbits = size.bit_length() - 1
    rounds = roots.shape[0]
    chans, rows = block.shape
    parts = next(p for p in (4, 2, 1) if rows % (p * size) == 0)
    if size & (size - 1) or rows % (parts * size) or nbits == 0:
        own = place == roots
        flipped = jnp.transpose(block)
        masked = jnp.where(own[:, None, None], flipped[None], jnp.zeros_like(flipped)[None])
        return lax.psum(masked, axis)
    piece = rows // (parts * size)
    orders = [[1 << ((p + s) % nbits) for s in range(nbits)] for p in range(parts)]
    bufs = {}
    for p in range(parts):
        seg = jnp.transpose(block[:, p * piece * size : (p + 1) * piece * size])
        seg = seg.reshape([2] * nbits + [piece, chans])
        perm = [nbits - 1 - (m.bit_length() - 1) for m in orders[p]] + [nbits, nbits + 1]
        seg = jnp.transpose(seg, perm)
        for r in range(rounds):
            bufs[p, r] = seg
    for s in range(nbits):
        sends, keeps = {}, {}
        for (p, r), buf in bufs.items():
            mask = orders[p][s]
            bit = (place // mask) % 2
            keeps[p, r] = jnp.where(bit == 1, buf[1], buf[0])
            sends.setdefault(mask, []).append(((p, r), jnp.where(bit == 1, buf[0], buf[1])))
        for mask, items in sorted(sends.items(), key=lambda kv: -kv[0]):
            got = lax.ppermute(jnp.stack([v for _, v in items]), axis, [(i, i ^ mask) for i in range(size)])
            for n, (key, _) in enumerate(items):
                held = sum(orders[key[0]][:s])
                holder = ((place ^ roots[key[1]]) & (size - 1 - held)) == 0
                bufs[key] = jnp.where(holder, keeps[key], got[n])
    for s in reversed(range(nbits)):
        sends = {}
        for (p, r), buf in bufs.items():
            sends.setdefault((r if s == 0 else 0, orders[p][s]), []).append(((p, r), buf))
        for (_, mask), items in sorted(sends.items(), key=lambda kv: (kv[0][0], -kv[0][1])):
            got = lax.ppermute(jnp.stack([v for _, v in items]), axis, [(i, i ^ mask) for i in range(size)])
            bit = (place // mask) % 2
            for n, (key, buf) in enumerate(items):
                low = jnp.where(bit == 1, got[n], buf)
                high = jnp.where(bit == 1, buf, got[n])
                bufs[key] = jnp.stack([low, high])
    out = []
    for r in range(rounds):
        segs = []
        for p in range(parts):
            perm = [nbits - 1 - (m.bit_length() - 1) for m in orders[p]]
            inverse = [perm.index(k) for k in range(nbits)] + [nbits, nbits + 1]
            segs.append(jnp.transpose(bufs[p, r], inverse).reshape(piece * size, chans))
        out.append(jnp.concatenate(segs, axis=0))
    return jnp.stack(out)


def correlate_kernel(meta_ref, blk_ref, ext_ref, corr_ref, power_ref):
    step = pl.program_id(0)
    chans = blk_ref.shape[2]
    width = ext_ref.shape[1]
    group = corr_ref.shape[1]
    lags = corr_ref.shape[2]
    tap = lax.broadcasted_iota(jnp.int32, (L, REACH), 0)
    col = lax.broadcasted_iota(jnp.int32, (L, REACH), 1)
    lane = lax.broadcasted_iota(jnp.int32, (L, chans), 1)
    pieces = []
    for g in range(group):
        idx = step * group + g
        first = meta_ref[4 * idx]
        shift = meta_ref[4 * idx + 1]
        lower = meta_ref[4 * idx + 2]
        upper = meta_ref[4 * idx + 3]
        rows = blk_ref[0, pl.ds(pl.multiple_of(first, 16), REACH), :]
        pick = (col == shift + (L - 1) - tap).astype(jnp.bfloat16)
        chosen = jnp.dot(pick, rows, preferred_element_type=jnp.float32)
        chosen = jnp.where((lane >= lower) & (lane < upper), chosen, 0.0)
        power_ref[0, g : g + 1, :] = jnp.full((1, 128), jnp.sum(chosen * chosen), jnp.float32)
        pieces.append(chosen.astype(jnp.bfloat16))
    product = jnp.dot(
        jnp.concatenate(pieces, axis=0), ext_ref[...], preferred_element_type=jnp.float32
    )
    for g in range(group):
        rows = product[g * L : (g + 1) * L]
        sheared = pltpu.roll(rows, width - (L - 1), 1, stride=1, stride_axis=0)
        corr_ref[0, g : g + 1, :] = jnp.sum(sheared, axis=0, keepdims=True)[:, :lags]


def correlate(meta, blocks, extended, count):
    rounds, span, chans = blocks.shape
    width = extended.shape[1]
    lag_count = span
    steps = rounds * count // GROUP
    per_round = count // GROUP
    cost = pl.CostEstimate(
        flops=2 * rounds * count * L * (chans * width + REACH * chans),
        transcendentals=0,
        bytes_accessed=blocks.size * 2 + extended.size * 2 + rounds * count * lag_count * 4,
    )
    grid_spec = pltpu.PrefetchScalarGridSpec(
        num_scalar_prefetch=1,
        grid=(steps,),
        in_specs=[
            pl.BlockSpec((1, span, chans), lambda i, m: (i // per_round, 0, 0)),
            pl.BlockSpec((chans, width), lambda i, m: (0, 0)),
        ],
        out_specs=[
            pl.BlockSpec((1, GROUP, lag_count), lambda i, m: (i, 0, 0)),
            pl.BlockSpec((1, GROUP, 128), lambda i, m: (i, 0, 0)),
        ],
    )
    corr, power = pl.pallas_call(
        correlate_kernel,
        grid_spec=grid_spec,
        out_shape=[
            jax.ShapeDtypeStruct((steps, GROUP, lag_count), jnp.float32),
            jax.ShapeDtypeStruct((steps, GROUP, 128), jnp.float32),
        ],
        cost_estimate=cost,
    )(meta, blocks, extended)
    return corr.reshape(rounds * count, lag_count), power[:, :, 0].reshape(rounds * count)


def window_sum(values, taps, lag_count):
    span = 1
    while span < taps:
        values = values[:, :-span] + values[:, span:]
        span *= 2
    return values[:, :lag_count]


def shards(signal, round_shard, offsets, chan_range):
    chan_local, lag_count = signal.shape
    rounds, count = offsets.shape
    section = lax.axis_index("sec")
    place = lax.axis_index("tm")
    total_lags = lag_count * lax.axis_size("tm")

    right_rim = from_behind(signal[:, :L], "tm", -1)
    extended = jnp.concatenate([signal, right_rim], axis=1)
    channel = section * chan_local + jnp.arange(chan_local, dtype=jnp.int32)
    lower = chan_range[:, :, 0]
    upper = chan_range[:, :, 1]
    inside = (channel >= lower[:, :, None]) & (channel < upper[:, :, None])

    blocks = spread_blocks(signal, round_shard, "tm")
    offs = jnp.clip(offsets, 0, lag_count - L)
    first = jnp.minimum((offs // 16) * 16, lag_count - REACH)
    base = section * chan_local
    meta = jnp.stack([first, offs - first, lower - base, upper - base], axis=-1).reshape(-1)

    squares = jnp.square(extended.astype(jnp.float32))
    high = lax.reduce_precision(squares, exponent_bits=8, mantissa_bits=7)
    low = (squares - high).astype(jnp.bfloat16)
    masks = inside.reshape(rounds * count, chan_local).astype(jnp.bfloat16)
    summed = jnp.dot(masks, high.astype(jnp.bfloat16), preferred_element_type=jnp.float32)
    summed = summed + jnp.dot(masks, low, preferred_element_type=jnp.float32)
    energy_local = window_sum(summed, L, lag_count)

    meta = meta.astype(jnp.int32).reshape(rounds, -1)
    pieces = [correlate(meta[r], blocks[r : r + 1], extended, count) for r in range(rounds)]
    corr_local = jnp.concatenate([c for c, _ in pieces])
    local_power = jnp.concatenate([p for _, p in pieces])
    tmpl_power = group_sum(local_power, "sec")
    both = group_sum(jnp.stack([corr_local, energy_local]), "sec")
    corr, energy = both[0], both[1]
    normed = corr / jnp.sqrt(energy * tmpl_power[:, None] + EPS)
    power_sum = group_sum(jnp.sum(normed * normed, axis=1), "tm")
    meansq = power_sum / total_lags
    scored = normed / jnp.sqrt(meansq[:, None] + EPS)
    return scored.reshape(rounds, count, lag_count)


def solution(mesh):
    placed = (P("sec", "tm"), P(), P(), P())
    return jax.shard_map(
        shards, mesh=mesh, in_specs=placed, out_specs=P(None, None, "tm"), check_vma=False
    )
```

```python
import jax
import jax.numpy as jnp
from jax import lax
from jax.experimental import pallas as pl
from jax.experimental.pallas import tpu as pltpu
from jax.sharding import PartitionSpec as P

L = 128
GROUP = 8
REACH = L + 16

EPS = 1e-06


def from_behind(value, axis, by):
    length = lax.axis_size(axis)
    pairs = [(i, i + by) for i in range(length) if 0 <= i + by < length]
    return lax.ppermute(value, axis, pairs)


def group_sum(value, axis):
    size = lax.axis_size(axis)
    place = lax.axis_index(axis)
    stride = 1
    while stride < size:
        fan = 4 if size % (stride * 4) == 0 else 2 if size % (stride * 2) == 0 else 0
        if fan == 0:
            return lax.psum(value, axis)
        member = (place // stride) % fan
        got = {0: value}
        for d in range(1, fan):
            pairs = [(i, i ^ (d * stride)) for i in range(size)]
            got[d] = lax.ppermute(value, axis, pairs)
        total = None
        for m in range(fan):
            part = got[0]
            for d in range(1, fan):
                part = jnp.where((member ^ d) == m, got[d], part)
            total = part if total is None else total + part
        value = total
        stride *= fan
    return value


def spread_blocks(block, roots, axis):
    size = lax.axis_size(axis)
    place = lax.axis_index(axis)
    nbits = size.bit_length() - 1
    rounds = roots.shape[0]
    chans, rows = block.shape
    parts = next(p for p in (4, 2, 1) if rows % (p * size) == 0)
    if size & (size - 1) or rows % (parts * size) or nbits == 0:
        own = place == roots
        flipped = jnp.transpose(block)
        masked = jnp.where(own[:, None, None], flipped[None], jnp.zeros_like(flipped)[None])
        return lax.psum(masked, axis)
    piece = rows // (parts * size)
    orders = [[1 << ((p + s) % nbits) for s in range(nbits)] for p in range(parts)]
    bufs = {}
    for p in range(parts):
        seg = jnp.transpose(block[:, p * piece * size : (p + 1) * piece * size])
        seg = seg.reshape([2] * nbits + [piece, chans])
        perm = [nbits - 1 - (m.bit_length() - 1) for m in orders[p]] + [nbits, nbits + 1]
        seg = jnp.transpose(seg, perm)
        for r in range(rounds):
            bufs[p, r] = seg
    for s in range(nbits):
        sends, keeps = {}, {}
        for (p, r), buf in bufs.items():
            mask = orders[p][s]
            bit = (place // mask) % 2
            keeps[p, r] = jnp.where(bit == 1, buf[1], buf[0])
            sends.setdefault(mask, []).append(((p, r), jnp.where(bit == 1, buf[0], buf[1])))
        for mask, items in sorted(sends.items(), key=lambda kv: -kv[0]):
            got = lax.ppermute(jnp.stack([v for _, v in items]), axis, [(i, i ^ mask) for i in range(size)])
            for n, (key, _) in enumerate(items):
                held = sum(orders[key[0]][:s])
                holder = ((place ^ roots[key[1]]) & (size - 1 - held)) == 0
                bufs[key] = jnp.where(holder, keeps[key], got[n])
    for s in reversed(range(nbits)):
        sends = {}
        for (p, r), buf in bufs.items():
            sends.setdefault((r if s == 0 else 0, orders[p][s]), []).append(((p, r), buf))
        for (_, mask), items in sorted(sends.items(), key=lambda kv: (kv[0][0], -kv[0][1])):
            got = lax.ppermute(jnp.stack([v for _, v in items]), axis, [(i, i ^ mask) for i in range(size)])
            bit = (place // mask) % 2
            for n, (key, buf) in enumerate(items):
                low = jnp.where(bit == 1, got[n], buf)
                high = jnp.where(bit == 1, buf, got[n])
                bufs[key] = jnp.stack([low, high])
    out = []
    for r in range(rounds):
        segs = []
        for p in range(parts):
            perm = [nbits - 1 - (m.bit_length() - 1) for m in orders[p]]
            inverse = [perm.index(k) for k in range(nbits)] + [nbits, nbits + 1]
            segs.append(jnp.transpose(bufs[p, r], inverse).reshape(piece * size, chans))
        out.append(jnp.concatenate(segs, axis=0))
    return jnp.stack(out)


def correlate_kernel(meta_ref, blk_ref, ext_ref, corr_ref, power_ref):
    step = pl.program_id(0)
    chans = blk_ref.shape[2]
    width = ext_ref.shape[1]
    group = corr_ref.shape[1]
    lags = corr_ref.shape[2]
    tap = lax.broadcasted_iota(jnp.int32, (L, REACH), 0)
    col = lax.broadcasted_iota(jnp.int32, (L, REACH), 1)
    lane = lax.broadcasted_iota(jnp.int32, (L, chans), 1)
    pieces = []
    for g in range(group):
        idx = step * group + g
        first = meta_ref[4 * idx]
        shift = meta_ref[4 * idx + 1]
        lower = meta_ref[4 * idx + 2]
        upper = meta_ref[4 * idx + 3]
        rows = blk_ref[0, pl.ds(pl.multiple_of(first, 16), REACH), :]
        pick = (col == shift + (L - 1) - tap).astype(jnp.bfloat16)
        chosen = jnp.dot(pick, rows, preferred_element_type=jnp.float32)
        chosen = jnp.where((lane >= lower) & (lane < upper), chosen, 0.0)
        power_ref[0, g : g + 1, :] = jnp.full((1, 128), jnp.sum(chosen * chosen), jnp.float32)
        pieces.append(chosen.astype(jnp.bfloat16))
    product = jnp.dot(
        jnp.concatenate(pieces, axis=0), ext_ref[...], preferred_element_type=jnp.float32
    )
    for g in range(group):
        rows = product[g * L : (g + 1) * L]
        sheared = pltpu.roll(rows, width - (L - 1), 1, stride=1, stride_axis=0)
        corr_ref[0, g : g + 1, :] = jnp.sum(sheared, axis=0, keepdims=True)[:, :lags]


def correlate(meta, blocks, extended, count):
    rounds, span, chans = blocks.shape
    width = extended.shape[1]
    lag_count = span
    steps = rounds * count // GROUP
    per_round = count // GROUP
    cost = pl.CostEstimate(
        flops=2 * rounds * count * L * (chans * width + REACH * chans),
        transcendentals=0,
        bytes_accessed=blocks.size * 2 + extended.size * 2 + rounds * count * lag_count * 4,
    )
    grid_spec = pltpu.PrefetchScalarGridSpec(
        num_scalar_prefetch=1,
        grid=(steps,),
        in_specs=[
            pl.BlockSpec((1, span, chans), lambda i, m: (i // per_round, 0, 0)),
            pl.BlockSpec((chans, width), lambda i, m: (0, 0)),
        ],
        out_specs=[
            pl.BlockSpec((1, GROUP, lag_count), lambda i, m: (i, 0, 0)),
            pl.BlockSpec((1, GROUP, 128), lambda i, m: (i, 0, 0)),
        ],
    )
    corr, power = pl.pallas_call(
        correlate_kernel,
        grid_spec=grid_spec,
        out_shape=[
            jax.ShapeDtypeStruct((steps, GROUP, lag_count), jnp.float32),
            jax.ShapeDtypeStruct((steps, GROUP, 128), jnp.float32),
        ],
        cost_estimate=cost,
    )(meta, blocks, extended)
    return corr.reshape(rounds * count, lag_count), power[:, :, 0].reshape(rounds * count)


def window_sum(values, taps, lag_count):
    span = 1
    while span < taps:
        values = values[:, :-span] + values[:, span:]
        span *= 2
    return values[:, :lag_count]


def shards(signal, round_shard, offsets, chan_range):
    chan_local, lag_count = signal.shape
    rounds, count = offsets.shape
    section = lax.axis_index("sec")
    place = lax.axis_index("tm")
    total_lags = lag_count * lax.axis_size("tm")

    right_rim = from_behind(signal[:, :L], "tm", -1)
    extended = jnp.concatenate([signal, right_rim], axis=1)
    channel = section * chan_local + jnp.arange(chan_local, dtype=jnp.int32)
    lower = chan_range[:, :, 0]
    upper = chan_range[:, :, 1]
    inside = (channel >= lower[:, :, None]) & (channel < upper[:, :, None])

    blocks = spread_blocks(signal, round_shard, "tm")
    offs = jnp.clip(offsets, 0, lag_count - L)
    first = jnp.minimum((offs // 16) * 16, lag_count - REACH)
    base = section * chan_local
    meta = jnp.stack([first, offs - first, lower - base, upper - base], axis=-1).reshape(-1)

    squares = jnp.square(extended.astype(jnp.float32))
    high = lax.reduce_precision(squares, exponent_bits=8, mantissa_bits=7)
    low = (squares - high).astype(jnp.bfloat16)
    masks = inside.reshape(rounds * count, chan_local).astype(jnp.bfloat16)
    summed = jnp.dot(masks, high.astype(jnp.bfloat16), preferred_element_type=jnp.float32)
    summed = summed + jnp.dot(masks, low, preferred_element_type=jnp.float32)
    energy_local = window_sum(summed, L, lag_count)

    meta = meta.astype(jnp.int32).reshape(rounds, -1)
    pieces = [correlate(meta[r], blocks[r : r + 1], extended, count) for r in range(rounds)]
    corr_local = jnp.concatenate([c for c, _ in pieces])
    local_power = jnp.concatenate([p for _, p in pieces])
    tmpl_power = group_sum(local_power, "sec")
    both = group_sum(jnp.stack([corr_local, energy_local]), "sec")
    corr, energy = both[0], both[1]
    normed = corr / jnp.sqrt(energy * tmpl_power[:, None] + EPS)
    power_sum = group_sum(jnp.sum(normed * normed, axis=1), "tm")
    meansq = power_sum / total_lags
    scored = normed / jnp.sqrt(meansq[:, None] + EPS)
    return scored.reshape(rounds, count, lag_count)


def solution(mesh):
    placed = (P("sec", "tm"), P(), P(), P())
    return jax.shard_map(
        shards, mesh=mesh, in_specs=placed, out_specs=P(None, None, "tm"), check_vma=False
    )
```

```python
import jax
import jax.numpy as jnp
from jax import lax
from jax.experimental import pallas as pl
from jax.experimental.pallas import tpu as pltpu
from jax.sharding import PartitionSpec as P

L = 128
GROUP = 4
REACH = L + 8

EPS = 1e-06


def from_behind(value, axis, by):
    length = lax.axis_size(axis)
    pairs = [(i, i + by) for i in range(length) if 0 <= i + by < length]
    return lax.ppermute(value, axis, pairs)


def group_sum(value, axis):
    size = lax.axis_size(axis)
    place = lax.axis_index(axis)
    stride = 1
    while stride < size:
        fan = 4 if size % (stride * 4) == 0 else 2 if size % (stride * 2) == 0 else 0
        if fan == 0:
            return lax.psum(value, axis)
        member = (place // stride) % fan
        got = {0: value}
        for d in range(1, fan):
            pairs = [(i, i ^ (d * stride)) for i in range(size)]
            got[d] = lax.ppermute(value, axis, pairs)
        total = None
        for m in range(fan):
            part = got[0]
            for d in range(1, fan):
                part = jnp.where((member ^ d) == m, got[d], part)
            total = part if total is None else total + part
        value = total
        stride *= fan
    return value


def spread_blocks(block, roots, axis):
    size = lax.axis_size(axis)
    place = lax.axis_index(axis)
    nbits = size.bit_length() - 1
    rounds = roots.shape[0]
    chans, rows = block.shape
    parts = next(p for p in (4, 2, 1) if rows % (p * size) == 0)
    if size & (size - 1) or rows % (parts * size) or nbits == 0:
        own = place == roots
        flipped = jnp.transpose(block)
        masked = jnp.where(own[:, None, None], flipped[None], jnp.zeros_like(flipped)[None])
        return lax.psum(masked, axis)
    piece = rows // (parts * size)
    orders = [[1 << ((p + s) % nbits) for s in range(nbits)] for p in range(parts)]
    bufs = {}
    for p in range(parts):
        seg = jnp.transpose(block[:, p * piece * size : (p + 1) * piece * size])
        seg = seg.reshape([2] * nbits + [piece, chans])
        perm = [nbits - 1 - (m.bit_length() - 1) for m in orders[p]] + [nbits, nbits + 1]
        seg = jnp.transpose(seg, perm)
        for r in range(rounds):
            bufs[p, r] = seg
    for s in range(nbits):
        sends, keeps = {}, {}
        for (p, r), buf in bufs.items():
            mask = orders[p][s]
            bit = (place // mask) % 2
            keeps[p, r] = jnp.where(bit == 1, buf[1], buf[0])
            sends.setdefault(mask, []).append(((p, r), jnp.where(bit == 1, buf[0], buf[1])))
        for mask, items in sorted(sends.items(), key=lambda kv: -kv[0]):
            got = lax.ppermute(jnp.stack([v for _, v in items]), axis, [(i, i ^ mask) for i in range(size)])
            for n, (key, _) in enumerate(items):
                held = sum(orders[key[0]][:s])
                holder = ((place ^ roots[key[1]]) & (size - 1 - held)) == 0
                bufs[key] = jnp.where(holder, keeps[key], got[n])
    for s in reversed(range(nbits)):
        sends = {}
        for (p, r), buf in bufs.items():
            sends.setdefault((r if s == 0 else 0, orders[p][s]), []).append(((p, r), buf))
        for (_, mask), items in sorted(sends.items(), key=lambda kv: (kv[0][0], -kv[0][1])):
            got = lax.ppermute(jnp.stack([v for _, v in items]), axis, [(i, i ^ mask) for i in range(size)])
            bit = (place // mask) % 2
            for n, (key, buf) in enumerate(items):
                low = jnp.where(bit == 1, got[n], buf)
                high = jnp.where(bit == 1, buf, got[n])
                bufs[key] = jnp.stack([low, high])
    out = []
    for r in range(rounds):
        segs = []
        for p in range(parts):
            perm = [nbits - 1 - (m.bit_length() - 1) for m in orders[p]]
            inverse = [perm.index(k) for k in range(nbits)] + [nbits, nbits + 1]
            segs.append(jnp.transpose(bufs[p, r], inverse).reshape(piece * size, chans))
        out.append(jnp.concatenate(segs, axis=0))
    return jnp.stack(out)


def correlate_kernel(meta_ref, blk_ref, ext_ref, corr_ref, power_ref):
    step = pl.program_id(0)
    chans = blk_ref.shape[2]
    width = ext_ref.shape[1]
    group = corr_ref.shape[1]
    lags = corr_ref.shape[2]
    tap = lax.broadcasted_iota(jnp.int32, (L, REACH), 0)
    col = lax.broadcasted_iota(jnp.int32, (L, REACH), 1)
    lane = lax.broadcasted_iota(jnp.int32, (L, chans), 1)
    pieces = []
    for g in range(group):
        idx = step * group + g
        first = meta_ref[4 * idx]
        shift = meta_ref[4 * idx + 1]
        lower = meta_ref[4 * idx + 2]
        upper = meta_ref[4 * idx + 3]
        rows = blk_ref[0, pl.ds(pl.multiple_of(first, 8), REACH), :]
        pick = (col == shift + (L - 1) - tap).astype(jnp.bfloat16)
        chosen = jnp.dot(pick, rows, preferred_element_type=jnp.float32)
        chosen = jnp.where((lane >= lower) & (lane < upper), chosen, 0.0)
        power_ref[0, g : g + 1, :] = jnp.full((1, 128), jnp.sum(chosen * chosen), jnp.float32)
        pieces.append(chosen.astype(jnp.bfloat16))
    product = jnp.dot(
        jnp.concatenate(pieces, axis=0), ext_ref[...], preferred_element_type=jnp.float32
    )
    for g in range(group):
        rows = product[g * L : (g + 1) * L]
        sheared = pltpu.roll(rows, width - (L - 1), 1, stride=1, stride_axis=0)
        corr_ref[0, g : g + 1, :] = jnp.sum(sheared, axis=0, keepdims=True)[:, :lags]


def correlate(meta, blocks, extended, count):
    rounds, span, chans = blocks.shape
    width = extended.shape[1]
    lag_count = span
    steps = rounds * count // GROUP
    per_round = count // GROUP
    cost = pl.CostEstimate(
        flops=2 * rounds * count * L * (chans * width + REACH * chans),
        transcendentals=0,
        bytes_accessed=blocks.size * 2 + extended.size * 2 + rounds * count * lag_count * 4,
    )
    grid_spec = pltpu.PrefetchScalarGridSpec(
        num_scalar_prefetch=1,
        grid=(steps,),
        in_specs=[
            pl.BlockSpec((1, span, chans), lambda i, m: (i // per_round, 0, 0)),
            pl.BlockSpec((chans, width), lambda i, m: (0, 0)),
        ],
        out_specs=[
            pl.BlockSpec((1, GROUP, lag_count), lambda i, m: (i, 0, 0)),
            pl.BlockSpec((1, GROUP, 128), lambda i, m: (i, 0, 0)),
        ],
    )
    corr, power = pl.pallas_call(
        correlate_kernel,
        grid_spec=grid_spec,
        out_shape=[
            jax.ShapeDtypeStruct((steps, GROUP, lag_count), jnp.float32),
            jax.ShapeDtypeStruct((steps, GROUP, 128), jnp.float32),
        ],
        cost_estimate=cost,
    )(meta, blocks, extended)
    return corr.reshape(rounds * count, lag_count), power[:, :, 0].reshape(rounds * count)


def window_sum(values, taps, lag_count):
    span = 1
    while span < taps:
        values = values[:, :-span] + values[:, span:]
        span *= 2
    return values[:, :lag_count]


def shards(signal, round_shard, offsets, chan_range):
    chan_local, lag_count = signal.shape
    rounds, count = offsets.shape
    section = lax.axis_index("sec")
    place = lax.axis_index("tm")
    total_lags = lag_count * lax.axis_size("tm")

    right_rim = from_behind(signal[:, :L], "tm", -1)
    extended = jnp.concatenate([signal, right_rim], axis=1)
    channel = section * chan_local + jnp.arange(chan_local, dtype=jnp.int32)
    lower = chan_range[:, :, 0]
    upper = chan_range[:, :, 1]
    inside = (channel >= lower[:, :, None]) & (channel < upper[:, :, None])

    blocks = spread_blocks(signal, round_shard, "tm")
    offs = jnp.clip(offsets, 0, lag_count - L)
    first = jnp.minimum((offs // 8) * 8, lag_count - REACH)
    base = section * chan_local
    meta = jnp.stack([first, offs - first, lower - base, upper - base], axis=-1).reshape(-1)

    squares = jnp.square(extended.astype(jnp.float32))
    high = lax.reduce_precision(squares, exponent_bits=8, mantissa_bits=7)
    low = (squares - high).astype(jnp.bfloat16)
    masks = inside.reshape(rounds * count, chan_local).astype(jnp.bfloat16)
    summed = jnp.dot(masks, high.astype(jnp.bfloat16), preferred_element_type=jnp.float32)
    summed = summed + jnp.dot(masks, low, preferred_element_type=jnp.float32)
    energy_local = window_sum(summed, L, lag_count)

    meta = meta.astype(jnp.int32).reshape(rounds, -1)
    pieces = [correlate(meta[r], blocks[r : r + 1], extended, count) for r in range(rounds)]
    corr_local = jnp.concatenate([c for c, _ in pieces])
    local_power = jnp.concatenate([p for _, p in pieces])
    tmpl_power = group_sum(local_power, "sec")
    both = group_sum(jnp.stack([corr_local, energy_local]), "sec")
    corr, energy = both[0], both[1]
    normed = corr / jnp.sqrt(energy * tmpl_power[:, None] + EPS)
    power_sum = group_sum(jnp.sum(normed * normed, axis=1), "tm")
    meansq = power_sum / total_lags
    scored = normed / jnp.sqrt(meansq[:, None] + EPS)
    return scored.reshape(rounds, count, lag_count)


def solution(mesh):
    placed = (P("sec", "tm"), P(), P(), P())
    return jax.shard_map(
        shards, mesh=mesh, in_specs=placed, out_specs=P(None, None, "tm"), check_vma=False
    )
```

```python
import jax
import jax.numpy as jnp
from jax import lax
from jax.experimental import pallas as pl
from jax.experimental.pallas import tpu as pltpu
from jax.sharding import PartitionSpec as P

L = 128
GROUP = 2
REACH = L + 16

EPS = 1e-06


def from_behind(value, axis, by):
    length = lax.axis_size(axis)
    pairs = [(i, i + by) for i in range(length) if 0 <= i + by < length]
    return lax.ppermute(value, axis, pairs)


def group_sum(value, axis):
    size = lax.axis_size(axis)
    place = lax.axis_index(axis)
    stride = 1
    while stride < size:
        fan = 4 if size % (stride * 4) == 0 else 2 if size % (stride * 2) == 0 else 0
        if fan == 0:
            return lax.psum(value, axis)
        member = (place // stride) % fan
        got = {0: value}
        for d in range(1, fan):
            pairs = [(i, i ^ (d * stride)) for i in range(size)]
            got[d] = lax.ppermute(value, axis, pairs)
        total = None
        for m in range(fan):
            part = got[0]
            for d in range(1, fan):
                part = jnp.where((member ^ d) == m, got[d], part)
            total = part if total is None else total + part
        value = total
        stride *= fan
    return value


def spread_blocks(block, roots, axis):
    size = lax.axis_size(axis)
    place = lax.axis_index(axis)
    nbits = size.bit_length() - 1
    rounds = roots.shape[0]
    chans, rows = block.shape
    parts = next(p for p in (4, 2, 1) if rows % (p * size) == 0)
    if size & (size - 1) or rows % (parts * size) or nbits == 0:
        own = place == roots
        flipped = jnp.transpose(block)
        masked = jnp.where(own[:, None, None], flipped[None], jnp.zeros_like(flipped)[None])
        return lax.psum(masked, axis)
    piece = rows // (parts * size)
    orders = [[1 << ((p + s) % nbits) for s in range(nbits)] for p in range(parts)]
    bufs = {}
    for p in range(parts):
        seg = jnp.transpose(block[:, p * piece * size : (p + 1) * piece * size])
        seg = seg.reshape([2] * nbits + [piece, chans])
        perm = [nbits - 1 - (m.bit_length() - 1) for m in orders[p]] + [nbits, nbits + 1]
        seg = jnp.transpose(seg, perm)
        for r in range(rounds):
            bufs[p, r] = seg
    for s in range(nbits):
        sends, keeps = {}, {}
        for (p, r), buf in bufs.items():
            mask = orders[p][s]
            bit = (place // mask) % 2
            keeps[p, r] = jnp.where(bit == 1, buf[1], buf[0])
            sends.setdefault(mask, []).append(((p, r), jnp.where(bit == 1, buf[0], buf[1])))
        for mask, items in sorted(sends.items(), key=lambda kv: -kv[0]):
            got = lax.ppermute(jnp.stack([v for _, v in items]), axis, [(i, i ^ mask) for i in range(size)])
            for n, (key, _) in enumerate(items):
                held = sum(orders[key[0]][:s])
                holder = ((place ^ roots[key[1]]) & (size - 1 - held)) == 0
                bufs[key] = jnp.where(holder, keeps[key], got[n])
    for s in reversed(range(nbits)):
        sends = {}
        for (p, r), buf in bufs.items():
            sends.setdefault((r if s == 0 else 0, orders[p][s]), []).append(((p, r), buf))
        for (_, mask), items in sorted(sends.items(), key=lambda kv: (kv[0][0], -kv[0][1])):
            got = lax.ppermute(jnp.stack([v for _, v in items]), axis, [(i, i ^ mask) for i in range(size)])
            bit = (place // mask) % 2
            for n, (key, buf) in enumerate(items):
                low = jnp.where(bit == 1, got[n], buf)
                high = jnp.where(bit == 1, buf, got[n])
                bufs[key] = jnp.stack([low, high])
    out = []
    for r in range(rounds):
        segs = []
        for p in range(parts):
            perm = [nbits - 1 - (m.bit_length() - 1) for m in orders[p]]
            inverse = [perm.index(k) for k in range(nbits)] + [nbits, nbits + 1]
            segs.append(jnp.transpose(bufs[p, r], inverse).reshape(piece * size, chans))
        out.append(jnp.concatenate(segs, axis=0))
    return jnp.stack(out)


def correlate_kernel(meta_ref, blk_ref, ext_ref, corr_ref, power_ref):
    step = pl.program_id(0)
    chans = blk_ref.shape[2]
    width = ext_ref.shape[1]
    group = corr_ref.shape[1]
    lags = corr_ref.shape[2]
    tap = lax.broadcasted_iota(jnp.int32, (L, REACH), 0)
    col = lax.broadcasted_iota(jnp.int32, (L, REACH), 1)
    lane = lax.broadcasted_iota(jnp.int32, (L, chans), 1)
    pieces = []
    for g in range(group):
        idx = step * group + g
        first = meta_ref[4 * idx]
        shift = meta_ref[4 * idx + 1]
        lower = meta_ref[4 * idx + 2]
        upper = meta_ref[4 * idx + 3]
        rows = blk_ref[0, pl.ds(pl.multiple_of(first, 16), REACH), :]
        pick = (col == shift + (L - 1) - tap).astype(jnp.bfloat16)
        chosen = jnp.dot(pick, rows, preferred_element_type=jnp.float32)
        chosen = jnp.where((lane >= lower) & (lane < upper), chosen, 0.0)
        power_ref[0, g : g + 1, :] = jnp.full((1, 128), jnp.sum(chosen * chosen), jnp.float32)
        pieces.append(chosen.astype(jnp.bfloat16))
    product = jnp.dot(
        jnp.concatenate(pieces, axis=0), ext_ref[...], preferred_element_type=jnp.float32
    )
    for g in range(group):
        rows = product[g * L : (g + 1) * L]
        sheared = pltpu.roll(rows, width - (L - 1), 1, stride=1, stride_axis=0)
        corr_ref[0, g : g + 1, :] = jnp.sum(sheared, axis=0, keepdims=True)[:, :lags]


def correlate(meta, blocks, extended, count):
    rounds, span, chans = blocks.shape
    width = extended.shape[1]
    lag_count = span
    steps = rounds * count // GROUP
    per_round = count // GROUP
    cost = pl.CostEstimate(
        flops=2 * rounds * count * L * (chans * width + REACH * chans),
        transcendentals=0,
        bytes_accessed=blocks.size * 2 + extended.size * 2 + rounds * count * lag_count * 4,
    )
    grid_spec = pltpu.PrefetchScalarGridSpec(
        num_scalar_prefetch=1,
        grid=(steps,),
        in_specs=[
            pl.BlockSpec((1, span, chans), lambda i, m: (i // per_round, 0, 0)),
            pl.BlockSpec((chans, width), lambda i, m: (0, 0)),
        ],
        out_specs=[
            pl.BlockSpec((1, GROUP, lag_count), lambda i, m: (i, 0, 0)),
            pl.BlockSpec((1, GROUP, 128), lambda i, m: (i, 0, 0)),
        ],
    )
    corr, power = pl.pallas_call(
        correlate_kernel,
        grid_spec=grid_spec,
        out_shape=[
            jax.ShapeDtypeStruct((steps, GROUP, lag_count), jnp.float32),
            jax.ShapeDtypeStruct((steps, GROUP, 128), jnp.float32),
        ],
        cost_estimate=cost,
    )(meta, blocks, extended)
    return corr.reshape(rounds * count, lag_count), power[:, :, 0].reshape(rounds * count)


def window_sum(values, taps, lag_count):
    span = 1
    while span < taps:
        values = values[:, :-span] + values[:, span:]
        span *= 2
    return values[:, :lag_count]


def shards(signal, round_shard, offsets, chan_range):
    chan_local, lag_count = signal.shape
    rounds, count = offsets.shape
    section = lax.axis_index("sec")
    place = lax.axis_index("tm")
    total_lags = lag_count * lax.axis_size("tm")

    right_rim = from_behind(signal[:, :L], "tm", -1)
    extended = jnp.concatenate([signal, right_rim], axis=1)
    channel = section * chan_local + jnp.arange(chan_local, dtype=jnp.int32)
    lower = chan_range[:, :, 0]
    upper = chan_range[:, :, 1]
    inside = (channel >= lower[:, :, None]) & (channel < upper[:, :, None])

    blocks = spread_blocks(signal, round_shard, "tm")
    offs = jnp.clip(offsets, 0, lag_count - L)
    first = jnp.minimum((offs // 16) * 16, lag_count - REACH)
    base = section * chan_local
    meta = jnp.stack([first, offs - first, lower - base, upper - base], axis=-1).reshape(-1)

    squares = jnp.square(extended.astype(jnp.float32))
    high = lax.reduce_precision(squares, exponent_bits=8, mantissa_bits=7)
    low = (squares - high).astype(jnp.bfloat16)
    masks = inside.reshape(rounds * count, chan_local).astype(jnp.bfloat16)
    summed = jnp.dot(masks, high.astype(jnp.bfloat16), preferred_element_type=jnp.float32)
    summed = summed + jnp.dot(masks, low, preferred_element_type=jnp.float32)
    energy_local = window_sum(summed, L, lag_count)

    meta = meta.astype(jnp.int32).reshape(rounds, -1)
    pieces = [correlate(meta[r], blocks[r : r + 1], extended, count) for r in range(rounds)]
    corr_local = jnp.concatenate([c for c, _ in pieces])
    local_power = jnp.concatenate([p for _, p in pieces])
    tmpl_power = group_sum(local_power, "sec")
    both = group_sum(jnp.stack([corr_local, energy_local]), "sec")
    corr, energy = both[0], both[1]
    normed = corr / jnp.sqrt(energy * tmpl_power[:, None] + EPS)
    power_sum = group_sum(jnp.sum(normed * normed, axis=1), "tm")
    meansq = power_sum / total_lags
    scored = normed / jnp.sqrt(meansq[:, None] + EPS)
    return scored.reshape(rounds, count, lag_count)


def solution(mesh):
    placed = (P("sec", "tm"), P(), P(), P())
    return jax.shard_map(
        shards, mesh=mesh, in_specs=placed, out_specs=P(None, None, "tm"), check_vma=False
    )
```

```python
import jax
import jax.numpy as jnp
from jax import lax
from jax.experimental import pallas as pl
from jax.experimental.pallas import tpu as pltpu
from jax.sharding import PartitionSpec as P

L = 128
GROUP = 4
REACH = L + 16

EPS = 1e-06


def from_behind(value, axis, by):
    length = lax.axis_size(axis)
    pairs = [(i, i + by) for i in range(length) if 0 <= i + by < length]
    return lax.ppermute(value, axis, pairs)


def group_sum(value, axis):
    size = lax.axis_size(axis)
    place = lax.axis_index(axis)
    stride = 1
    while stride < size:
        fan = 4 if size % (stride * 4) == 0 else 2 if size % (stride * 2) == 0 else 0
        if fan == 0:
            return lax.psum(value, axis)
        member = (place // stride) % fan
        got = {0: value}
        for d in range(1, fan):
            pairs = [(i, i ^ (d * stride)) for i in range(size)]
            got[d] = lax.ppermute(value, axis, pairs)
        total = None
        for m in range(fan):
            part = got[0]
            for d in range(1, fan):
                part = jnp.where((member ^ d) == m, got[d], part)
            total = part if total is None else total + part
        value = total
        stride *= fan
    return value


def spread_blocks(block, roots, axis, later=None):
    size = lax.axis_size(axis)
    place = lax.axis_index(axis)
    nbits = size.bit_length() - 1
    rounds = roots.shape[0]
    chans, rows = block.shape
    parts = next(p for p in (4, 2, 1) if rows % (p * size) == 0)
    if size & (size - 1) or rows % (parts * size) or nbits == 0:
        own = place == roots
        flipped = jnp.transpose(block)
        masked = jnp.where(own[:, None, None], flipped[None], jnp.zeros_like(flipped)[None])
        return lax.psum(masked, axis), later
    piece = rows // (parts * size)
    orders = [[1 << ((p + s) % nbits) for s in range(nbits)] for p in range(parts)]
    bufs = {}
    for p in range(parts):
        seg = jnp.transpose(block[:, p * piece * size : (p + 1) * piece * size])
        seg = seg.reshape([2] * nbits + [piece, chans])
        perm = [nbits - 1 - (m.bit_length() - 1) for m in orders[p]] + [nbits, nbits + 1]
        seg = jnp.transpose(seg, perm)
        for r in range(rounds):
            bufs[p, r] = seg
    for s in range(nbits):
        sends, keeps = {}, {}
        for (p, r), buf in bufs.items():
            mask = orders[p][s]
            bit = (place // mask) % 2
            keeps[p, r] = jnp.where(bit == 1, buf[1], buf[0])
            sends.setdefault(mask, []).append(((p, r), jnp.where(bit == 1, buf[0], buf[1])))
        for mask, items in sorted(sends.items(), key=lambda kv: -kv[0]):
            got = lax.ppermute(jnp.stack([v for _, v in items]), axis, [(i, i ^ mask) for i in range(size)])
            for n, (key, _) in enumerate(items):
                held = sum(orders[key[0]][:s])
                holder = ((place ^ roots[key[1]]) & (size - 1 - held)) == 0
                bufs[key] = jnp.where(holder, keeps[key], got[n])
        if s == 0:
            keys = sorted(bufs)
            vals, later = lax.optimization_barrier(([bufs[k] for k in keys], later))
            bufs = dict(zip(keys, vals))
    for s in reversed(range(nbits)):
        sends = {}
        for (p, r), buf in bufs.items():
            sends.setdefault((r if s == 0 else 0, orders[p][s]), []).append(((p, r), buf))
        for (_, mask), items in sorted(sends.items(), key=lambda kv: (kv[0][0], -kv[0][1])):
            got = lax.ppermute(jnp.stack([v for _, v in items]), axis, [(i, i ^ mask) for i in range(size)])
            bit = (place // mask) % 2
            for n, (key, buf) in enumerate(items):
                low = jnp.where(bit == 1, got[n], buf)
                high = jnp.where(bit == 1, buf, got[n])
                bufs[key] = jnp.stack([low, high])
    out = []
    for r in range(rounds):
        segs = []
        for p in range(parts):
            perm = [nbits - 1 - (m.bit_length() - 1) for m in orders[p]]
            inverse = [perm.index(k) for k in range(nbits)] + [nbits, nbits + 1]
            segs.append(jnp.transpose(bufs[p, r], inverse).reshape(piece * size, chans))
        out.append(jnp.concatenate(segs, axis=0))
    return jnp.stack(out), later


def correlate_kernel(meta_ref, blk_ref, ext_ref, corr_ref, power_ref):
    step = pl.program_id(0)
    chans = blk_ref.shape[2]
    width = ext_ref.shape[1]
    group = corr_ref.shape[1]
    lags = corr_ref.shape[2]
    tap = lax.broadcasted_iota(jnp.int32, (L, REACH), 0)
    col = lax.broadcasted_iota(jnp.int32, (L, REACH), 1)
    lane = lax.broadcasted_iota(jnp.int32, (L, chans), 1)
    pieces = []
    for g in range(group):
        idx = step * group + g
        first = meta_ref[4 * idx]
        shift = meta_ref[4 * idx + 1]
        lower = meta_ref[4 * idx + 2]
        upper = meta_ref[4 * idx + 3]
        rows = blk_ref[0, pl.ds(pl.multiple_of(first, 16), REACH), :]
        pick = (col == shift + (L - 1) - tap).astype(jnp.bfloat16)
        chosen = jnp.dot(pick, rows, preferred_element_type=jnp.float32)
        chosen = jnp.where((lane >= lower) & (lane < upper), chosen, 0.0)
        power_ref[0, g : g + 1, :] = jnp.full((1, 128), jnp.sum(chosen * chosen), jnp.float32)
        pieces.append(chosen.astype(jnp.bfloat16))
    product = jnp.dot(
        jnp.concatenate(pieces, axis=0), ext_ref[...], preferred_element_type=jnp.float32
    )
    for g in range(group):
        rows = product[g * L : (g + 1) * L]
        sheared = pltpu.roll(rows, width - (L - 1), 1, stride=1, stride_axis=0)
        corr_ref[0, g : g + 1, :] = jnp.sum(sheared, axis=0, keepdims=True)[:, :lags]


def correlate(meta, blocks, extended, count):
    rounds, span, chans = blocks.shape
    width = extended.shape[1]
    lag_count = span
    steps = rounds * count // GROUP
    per_round = count // GROUP
    cost = pl.CostEstimate(
        flops=2 * rounds * count * L * (chans * width + REACH * chans),
        transcendentals=0,
        bytes_accessed=blocks.size * 2 + extended.size * 2 + rounds * count * lag_count * 4,
    )
    grid_spec = pltpu.PrefetchScalarGridSpec(
        num_scalar_prefetch=1,
        grid=(steps,),
        in_specs=[
            pl.BlockSpec((1, span, chans), lambda i, m: (i // per_round, 0, 0)),
            pl.BlockSpec((chans, width), lambda i, m: (0, 0)),
        ],
        out_specs=[
            pl.BlockSpec((1, GROUP, lag_count), lambda i, m: (i, 0, 0)),
            pl.BlockSpec((1, GROUP, 128), lambda i, m: (i, 0, 0)),
        ],
    )
    corr, power = pl.pallas_call(
        correlate_kernel,
        grid_spec=grid_spec,
        out_shape=[
            jax.ShapeDtypeStruct((steps, GROUP, lag_count), jnp.float32),
            jax.ShapeDtypeStruct((steps, GROUP, 128), jnp.float32),
        ],
        cost_estimate=cost,
    )(meta, blocks, extended)
    return corr.reshape(rounds * count, lag_count), power[:, :, 0].reshape(rounds * count)


def window_sum(values, taps, lag_count):
    span = 1
    while span < taps:
        values = values[:, :-span] + values[:, span:]
        span *= 2
    return values[:, :lag_count]


def shards(signal, round_shard, offsets, chan_range):
    chan_local, lag_count = signal.shape
    rounds, count = offsets.shape
    section = lax.axis_index("sec")
    place = lax.axis_index("tm")
    total_lags = lag_count * lax.axis_size("tm")

    right_rim = from_behind(signal[:, :L], "tm", -1)
    extended = jnp.concatenate([signal, right_rim], axis=1)
    channel = section * chan_local + jnp.arange(chan_local, dtype=jnp.int32)
    lower = chan_range[:, :, 0]
    upper = chan_range[:, :, 1]
    inside = (channel >= lower[:, :, None]) & (channel < upper[:, :, None])

    blocks, extended = spread_blocks(signal, round_shard, "tm", extended)
    offs = jnp.clip(offsets, 0, lag_count - L)
    first = jnp.minimum((offs // 16) * 16, lag_count - REACH)
    base = section * chan_local
    meta = jnp.stack([first, offs - first, lower - base, upper - base], axis=-1).reshape(-1)

    squares = jnp.square(extended.astype(jnp.float32))
    high = lax.reduce_precision(squares, exponent_bits=8, mantissa_bits=7)
    low = (squares - high).astype(jnp.bfloat16)
    masks = inside.reshape(rounds * count, chan_local).astype(jnp.bfloat16)
    summed = jnp.dot(masks, high.astype(jnp.bfloat16), preferred_element_type=jnp.float32)
    summed = summed + jnp.dot(masks, low, preferred_element_type=jnp.float32)
    energy_local = window_sum(summed, L, lag_count)

    meta = meta.astype(jnp.int32).reshape(rounds, -1)
    pieces = [correlate(meta[r], blocks[r : r + 1], extended, count) for r in range(rounds)]
    corr_local = jnp.concatenate([c for c, _ in pieces])
    local_power = jnp.concatenate([p for _, p in pieces])
    tmpl_power = group_sum(local_power, "sec")
    both = group_sum(jnp.stack([corr_local, energy_local]), "sec")
    corr, energy = both[0], both[1]
    normed = corr / jnp.sqrt(energy * tmpl_power[:, None] + EPS)
    power_sum = group_sum(jnp.sum(normed * normed, axis=1), "tm")
    meansq = power_sum / total_lags
    scored = normed / jnp.sqrt(meansq[:, None] + EPS)
    return scored.reshape(rounds, count, lag_count)


def solution(mesh):
    placed = (P("sec", "tm"), P(), P(), P())
    return jax.shard_map(
        shards, mesh=mesh, in_specs=placed, out_specs=P(None, None, "tm"), check_vma=False
    )
```
